512 devices in a mesh: area: 128 (over z, y, core), blk: 4 (over x).
Axes of the slice: x: 4, y: 8, z: 8, core: 2. Of those that a mesh axis runs over, the one named last changes fastest.
Arguments:
- activity: float32 [1024, 4, 64, 128], P('area', 'blk'), may hold values from -8 to 8
- ext_input: bfloat16 [1024, 4, 64, 128], P('area', 'blk'), may hold values from -5 to 5
- weights: bfloat16 [384, 4, 128, 512], P('area', 'blk'), may hold values from -0.25 to 0.25
- slot_dst: int32 [384], P('area'), may hold values from 0 to 7
- slot_src: int32 [384], P('area'), may hold values from 0 to 1023, as said below
- slot_count: int32 [128], P('area'), may hold values from 3 to 3, as said below
- hebb_mask: int32 [384], P('area'), may hold values 0 or 1
Outputs:
- final_activity: float32 [1024, 4, 64, 128], P('area', 'blk')
- plasticity: bfloat16 [384, 4, 128, 512], P('area', 'blk')
The draws below stay inside these ranges and needn't reach their ends.
Inputs may be any that keep to these rules, and one draw needn't show every extreme that they name: Index i of area holds area i // 4; sources lie in areas listed for it by a connectome over the areas that always lists the area itself, the areas beside it on both sides (counted round) and the opposite one. Slots 0, 1 and 2 of index i of area have their source sub-blocks held by indices (i - 1) mod 128, (i + 1) mod 128 and (i + 64) mod 128. Among the occupied slots of one index of area, at most 1 have source sub-blocks held by one index of area (slot_src // 8); some index of area reaches 1. `slot_count`: some index of area has all 3 slots occupied.
All inputs are finite; a program needn't handle non-finite values. No bound on the sum of `hebb_mask` on one device may be relied on, other than what follows from the above.
Results may differ from the reference program's by a relative error of at most 0.014.
Values may be sent and summed in bfloat16 or wider, within the bound.
No kernel may reach another device: no remote copies, remote signals or barrier semaphores. Data moves between devices by JAX's collectives and lax.ppermute only.
A program may use at most 64 MiB of HBM per device.

```python
import jax
import jax.numpy as jnp
from jax import lax

SUB = 512
SPLIT = 4
TRIALS = 64
STEPS = 4
CAP = 3
SUB_DEV = 8
QW = 128
NSUB = 1024
SLOTS = 384
N_AREA = 128
N_BLK = 4


def draw_slot_src(key, part):
    n_areas = N_AREA // SPLIT
    listed = jax.random.randint(jax.random.fold_in(key, 13), (n_areas, n_areas), 0, 3) < 2
    forced_span = (CAP + SPLIT - 1) // SPLIT
    gap_areas = (jnp.arange(n_areas)[None, :] - jnp.arange(n_areas)[:, None]) % n_areas
    listed = listed | (gap_areas < forced_span) | (gap_areas == n_areas // 2) | (gap_areas == 1) | (gap_areas == n_areas - 1)
    owner_area = jnp.arange(N_AREA) // SPLIT
    owner_listed = listed[owner_area][:, owner_area].astype(jnp.int32)
    row_keys = jax.random.split(jax.random.fold_in(key, 11), N_AREA)

    def one_order(row_lookup_key):
        return jax.random.permutation(row_lookup_key, N_AREA)
    orders = jax.vmap(one_order)(row_keys).astype(jnp.int32)
    own_index = jnp.arange(N_AREA)
    prev_owner = (own_index + N_AREA - 1) % N_AREA
    next_owner = (own_index + 1) % N_AREA
    far_owner = (own_index + N_AREA // 2) % N_AREA
    is_prev = (own_index[None, :] == prev_owner[:, None]).astype(jnp.int32)
    is_next = (own_index[None, :] == next_owner[:, None]).astype(jnp.int32)
    is_far = (own_index[None, :] == far_owner[:, None]).astype(jnp.int32)
    scores = orders + N_AREA * (1 - owner_listed) - 4 * N_AREA * is_prev - 3 * N_AREA * is_next - 2 * N_AREA * is_far
    sorted_owners = jnp.argsort(scores, axis=1, stable=True).astype(jnp.int32)
    n_listed = jnp.sum(owner_listed, axis=1)
    pick_pos = (jnp.arange(CAP)[None, :] % n_listed[:, None]).astype(jnp.int32)
    owner_idx = jnp.take_along_axis(sorted_owners, pick_pos, axis=1)
    local_idx = jax.random.randint(jax.random.fold_in(key, 12), (N_AREA, CAP), 0, SUB_DEV)
    return (owner_idx * SUB_DEV + local_idx).reshape(N_AREA * CAP).astype(jnp.int32)


def draw_slot_count(key, part):
    first_draw = jax.random.randint(jax.random.fold_in(key, 21), (N_AREA,), 0, CAP)
    second_draw = jax.random.randint(jax.random.fold_in(key, 22), (N_AREA,), 0, CAP)
    counts = jnp.minimum(3 + first_draw * second_draw // CAP, CAP)
    chosen = jax.random.randint(jax.random.fold_in(key, 23), (), 0, N_AREA)
    return jnp.where(jnp.arange(N_AREA) == chosen, CAP, counts).astype(jnp.int32)


def set_ends(values, stream_key, smallest, largest):
    longest = values.shape.index(max(values.shape))
    spots = []
    for shift in (0, 1):
        where = [jax.random.randint(jax.random.fold_in(stream_key, axis), (), 0, length) for axis, length in enumerate(values.shape)]
        where[longest] = (where[longest] + shift) % values.shape[longest]
        spots.append(tuple(where))
    return values.at[spots[0]].set(smallest).at[spots[1]].set(largest)


def block_scale(rng, shape, cuts, low, high):
    def one(axis_at, shards_of):
        heights = jax.random.uniform(jax.random.fold_in(jax.random.fold_in(rng, 6), axis_at), (shards_of,), jnp.float32, low / len(cuts), high / len(cuts))
        return jnp.repeat(jnp.exp(heights), shape[axis_at] // shards_of).reshape((-1,) + (1,) * (len(shape) - axis_at - 1))

    level = one(*cuts[0])
    for cut in cuts[1:]:
        level = level * one(*cut)
    return level


def gaussian(own_key, extent, scale, limit, pieces=(), kind=jnp.bfloat16):
    values = jax.random.normal(own_key, extent, jnp.float32) * scale
    if len(pieces) > 0:
        values = block_scale(own_key, extent, pieces, -0.22, 0.18) * values
    return jnp.clip(values, min=-limit, max=limit).astype(kind)


def setup_inputs(seed: int = 0) -> dict:
    arg_keys = jax.random.split(jax.random.key(seed), 8)
    activity = gaussian(arg_keys[0], (NSUB, N_BLK, TRIALS, QW), 1.5, 8.0, ((0, 128), (1, 4)), jnp.float32)
    ext_input = gaussian(arg_keys[1], (NSUB, N_BLK, TRIALS, QW), 0.7, 5.0, ((0, 128), (1, 4)))
    weights = gaussian(arg_keys[2], (SLOTS, N_BLK, QW, SUB), SUB ** -0.5, 0.25, ((0, 128), (1, 4)))
    slot_dst = set_ends(jax.random.randint(arg_keys[3], (SLOTS,), 0, SUB_DEV), jax.random.fold_in(arg_keys[3], 1), 0, SUB_DEV - 1).astype(jnp.int32)
    slot_src = draw_slot_src(jax.random.fold_in(arg_keys[7], 71), 0)
    slot_count = draw_slot_count(jax.random.fold_in(arg_keys[7], 71), 0)
    hebb_mask = set_ends((jax.random.randint(arg_keys[6], (SLOTS,), 0, 4) < 3).astype(jnp.int32), jax.random.fold_in(arg_keys[6], 1), 0, 1)
    return dict(activity=activity, ext_input=ext_input, weights=weights, slot_dst=slot_dst, slot_src=slot_src, slot_count=slot_count, hebb_mask=hebb_mask)


euler_step = 0.5


def reference(activity, ext_input, weights, slot_dst, slot_src, slot_count, hebb_mask):
    n_subs, n_parts, trials, quarter = activity.shape
    sub_width = n_parts * quarter
    occupied = (jnp.arange(CAP)[None, :] < slot_count[:, None])
    src_rows = slot_src.reshape(N_AREA, CAP)
    dst_local = slot_dst.reshape(N_AREA, CAP)
    w_holders = weights.reshape(N_AREA, CAP, n_parts, quarter, sub_width)

    def inputs_of(rate_now):
        def holder_inputs(packed):
            w_slot, src_here, dst_here, occ_here = packed
            presynaptic_rates = rate_now[src_here].astype(jnp.float32)
            input_contribution = jnp.einsum("kjtq,kjqs->kjts", presynaptic_rates, w_slot.astype(jnp.float32), precision=lax.Precision.HIGHEST)
            select = ((dst_here[:, None] == jnp.arange(SUB_DEV)[None, :]) & occ_here[:, None]).astype(jnp.float32)
            partial_value = jnp.einsum("kd,kjts->jdts", select, input_contribution, precision=lax.Precision.HIGHEST)
            partial_value = lax.optimization_barrier(partial_value.astype(jnp.bfloat16)).astype(jnp.float32)
            summed = jnp.sum(partial_value, axis=0)
            return summed.reshape(SUB_DEV, trials, n_parts, quarter).transpose(0, 2, 1, 3)

        result = lax.map(holder_inputs, (w_holders, src_rows, dst_local, occupied))
        return result.reshape(n_subs, n_parts, trials, quarter)

    current = activity
    drive_in = ext_input.astype(jnp.float32)
    rate_now = jnp.tanh(current).astype(jnp.bfloat16)
    rate_list = [rate_now]
    for step_idx in range(STEPS):
        current = current + euler_step * (inputs_of(rate_now) - current + drive_in)
        rate_now = jnp.tanh(current).astype(jnp.bfloat16)
        rate_list.append(rate_now)
    stacked = jnp.stack(rate_list).astype(jnp.float32)
    centered = (stacked - jnp.mean(stacked, axis=3, keepdims=True)).astype(jnp.bfloat16)
    pre_all = centered[:STEPS]
    post_all = centered[1:]
    gates = (occupied & (hebb_mask.reshape(N_AREA, CAP) == 1)).astype(jnp.float32)
    dst_global = (jnp.arange(N_AREA)[:, None] * SUB_DEV + dst_local).astype(jnp.int32)
    norm_scale = (STEPS * trials) ** -0.5

    def holder_update(packed):
        src_here, dst_here, gate_on = packed
        presynaptic_rates = pre_all[:, src_here].astype(jnp.float32)
        postsynaptic_whole = post_all[:, dst_here].transpose(0, 1, 3, 2, 4).reshape(STEPS, CAP, trials, sub_width).astype(jnp.float32)
        change = jnp.einsum("tkjnq,tkns->kjqs", presynaptic_rates, postsynaptic_whole, precision=lax.Precision.HIGHEST)
        return (change * gate_on[:, None, None, None] * norm_scale).astype(jnp.bfloat16)

    plasticity = lax.map(holder_update, (src_rows, dst_global, gates))
    return current, plasticity.reshape(N_AREA * CAP, n_parts, quarter, sub_width)
```

```python
import jax
import jax.numpy as jnp
from jax import lax
from jax.sharding import PartitionSpec as P

STEPS = 4


euler_step = 0.5


def centre(x):
    xf = x.astype(jnp.float32)
    return (xf - jnp.mean(xf, axis=-2, keepdims=True)).astype(jnp.bfloat16)


def body(activity, ext_input, weights, slot_dst, slot_src, slot_count, hebb_mask):
    n_areas = lax.axis_size("area")
    n_blk = lax.axis_size("blk")
    my_blk = lax.axis_index("blk")
    sub_dev = activity.shape[0]
    trials = activity.shape[2]
    quarter = activity.shape[3]
    slot_cap = slot_src.shape[0]
    sub_width = weights.shape[3]
    offsets = (-1, 1, n_areas // 2)

    occupied = jnp.arange(slot_cap) < slot_count[0]
    select = ((slot_dst[:, None] == jnp.arange(sub_dev)[None, :]) & occupied[:, None]).astype(jnp.float32)

    wanted = jnp.clip(slot_src % sub_dev, 0, sub_dev - 1).astype(jnp.int32)
    provide = []
    for k in range(slot_cap):
        perm = [(i, (i + offsets[k]) % n_areas) for i in range(n_areas)]
        provide.append(lax.ppermute(wanted[k], "area", perm))

    w_split = weights[:, 0].reshape(slot_cap, quarter, n_blk, quarter)
    w_parts = lax.all_to_all(w_split, "blk", split_axis=2, concat_axis=2, tiled=True)
    part_of_shift = (my_blk - jnp.arange(n_blk)) % n_blk
    w_shift = jnp.take(w_parts, part_of_shift, axis=2).transpose(0, 2, 1, 3)

    def n_of(area_idx, blk_idx):
        return area_idx * n_blk + blk_idx

    def exchange(rate_own):
        got = []
        for k in range(slot_cap):
            payload = lax.dynamic_index_in_dim(rate_own, provide[k], 0, keepdims=False)
            per_shift = []
            for s in range(n_blk):
                perm = [
                    (n_of(i, b), n_of((i - offsets[k]) % n_areas, (b + s) % n_blk))
                    for i in range(n_areas)
                    for b in range(n_blk)
                ]
                per_shift.append(lax.ppermute(payload, ("area", "blk"), perm))
            got.append(jnp.stack(per_shift))
        return jnp.stack(got)

    current = activity[:, 0]
    drive_in = ext_input[:, 0].astype(jnp.float32)
    rate_own = jnp.tanh(current).astype(jnp.bfloat16)
    pre_list = []
    post_list = []
    for step_idx in range(STEPS):
        presyn = exchange(rate_own)
        contrib = jnp.einsum("ksnq,ksqv->ksnv", presyn, w_shift, preferred_element_type=jnp.float32)
        partial_value = jnp.einsum("kd,ksnv->sdnv", select, contrib, precision=lax.Precision.HIGHEST)
        summed = jnp.sum(partial_value.astype(jnp.bfloat16).astype(jnp.float32), axis=0)
        current = current + euler_step * (summed - current + drive_in)
        rate_own = jnp.tanh(current).astype(jnp.bfloat16)
        pre_list.append(presyn[:, 0])
        post_list.append(rate_own)
    final_state = current[:, None]

    pre_centered = centre(jnp.stack(pre_list, axis=1))
    post_centered = centre(jnp.stack(post_list, axis=0))
    post_sel = jnp.take(post_centered, slot_dst, axis=1).transpose(1, 0, 2, 3)
    post_whole = lax.all_gather(post_sel, "blk", axis=3, tiled=True)
    change = jnp.einsum("ktnq,ktnu->kqu", pre_centered, post_whole, preferred_element_type=jnp.float32)
    gate_on = (occupied & (hebb_mask == 1)).astype(jnp.float32)
    norm_scale = (STEPS * trials) ** (-0.5)
    plasticity = (change * gate_on[:, None, None] * norm_scale).astype(jnp.bfloat16)[:, None]
    return (final_state, plasticity)


def solution(mesh):
    in_specs = (
        P("area", "blk", None, None),
        P("area", "blk", None, None),
        P("area", "blk", None, None),
        P("area"),
        P("area"),
        P("area"),
        P("area"),
    )
    out_specs = (P("area", "blk", None, None), P("area", "blk", None, None))
    return jax.shard_map(body, mesh=mesh, in_specs=in_specs, out_specs=out_specs, check_vma=False)
```

```python
import jax
import jax.numpy as jnp
from jax import lax
from jax.sharding import PartitionSpec as P

STEPS = 4


euler_step = 0.5


def centre(x):
    xf = x.astype(jnp.float32)
    return (xf - jnp.mean(xf, axis=-2, keepdims=True)).astype(jnp.bfloat16)


def body(activity, ext_input, weights, slot_dst, slot_src, slot_count, hebb_mask):
    n_areas = lax.axis_size("area")
    my_blk = lax.axis_index("blk")
    sub_dev = activity.shape[0]
    trials = activity.shape[2]
    quarter = activity.shape[3]
    slot_cap = slot_src.shape[0]
    sub_width = weights.shape[3]
    n_parts = sub_width // quarter
    offsets = (-1, 1, n_areas // 2)

    occupied = jnp.arange(slot_cap) < slot_count[0]
    select = ((slot_dst[:, None] == jnp.arange(sub_dev)[None, :]) & occupied[:, None]).astype(jnp.float32)

    wanted = jnp.clip(slot_src % sub_dev, 0, sub_dev - 1).astype(jnp.int32)
    provide = []
    for k in range(slot_cap):
        perm = [(i, (i + offsets[k]) % n_areas) for i in range(n_areas)]
        provide.append(lax.ppermute(wanted[k], "area", perm))

    w_full = lax.all_gather(weights[:, 0], "blk", axis=1, tiled=False)
    act_full = lax.all_gather(activity[:, 0], "blk", axis=1, tiled=False)
    ext_full = lax.all_gather(ext_input[:, 0], "blk", axis=1, tiled=False)
    current = act_full.transpose(0, 2, 1, 3).reshape(sub_dev, trials, sub_width)
    drive_in = ext_full.transpose(0, 2, 1, 3).reshape(sub_dev, trials, sub_width).astype(jnp.float32)

    def exchange(rate_full):
        got = []
        for k in range(slot_cap):
            payload = lax.dynamic_index_in_dim(rate_full, provide[k], 0, keepdims=False)
            perm = [(i, (i - offsets[k]) % n_areas) for i in range(n_areas)]
            got.append(lax.ppermute(payload, "area", perm))
        return jnp.stack(got)

    rate_full = jnp.tanh(current).astype(jnp.bfloat16)
    pre_list = []
    post_list = []
    for step_idx in range(STEPS):
        presyn = exchange(rate_full)
        presyn_parts = presyn.reshape(slot_cap, trials, n_parts, quarter)
        contrib = jnp.einsum("knjq,kjqv->kjnv", presyn_parts, w_full, preferred_element_type=jnp.float32)
        partial_value = jnp.einsum("kd,kjnv->jdnv", select, contrib, precision=lax.Precision.HIGHEST)
        summed = jnp.sum(partial_value.astype(jnp.bfloat16).astype(jnp.float32), axis=0)
        current = current + euler_step * (summed - current + drive_in)
        rate_full = jnp.tanh(current).astype(jnp.bfloat16)
        pre_list.append(lax.dynamic_slice_in_dim(presyn, my_blk * quarter, quarter, 2))
        post_list.append(rate_full)
    final_state = lax.dynamic_slice_in_dim(current, my_blk * quarter, quarter, 2)[:, None]

    pre_centered = centre(jnp.stack(pre_list, axis=1))
    post_centered = centre(jnp.stack(post_list, axis=0))
    post_sel = jnp.take(post_centered, slot_dst, axis=1).transpose(1, 0, 2, 3)
    change = jnp.einsum("ktnq,ktnu->kqu", pre_centered, post_sel, preferred_element_type=jnp.float32)
    gate_on = (occupied & (hebb_mask == 1)).astype(jnp.float32)
    norm_scale = (STEPS * trials) ** (-0.5)
    plasticity = (change * gate_on[:, None, None] * norm_scale).astype(jnp.bfloat16)[:, None]
    return (final_state, plasticity)


def solution(mesh):
    in_specs = (
        P("area", "blk", None, None),
        P("area", "blk", None, None),
        P("area", "blk", None, None),
        P("area"),
        P("area"),
        P("area"),
        P("area"),
    )
    out_specs = (P("area", "blk", None, None), P("area", "blk", None, None))
    return jax.shard_map(body, mesh=mesh, in_specs=in_specs, out_specs=out_specs, check_vma=False)
```

```python
import jax
import jax.numpy as jnp
from jax import lax
from jax.sharding import PartitionSpec as P

STEPS = 4


euler_step = 0.5


def centre(x):
    xf = x.astype(jnp.float32)
    return (xf - jnp.mean(xf, axis=-2, keepdims=True)).astype(jnp.bfloat16)


def body(activity, ext_input, weights, slot_dst, slot_src, slot_count, hebb_mask):
    n_areas = lax.axis_size("area")
    my_blk = lax.axis_index("blk")
    sub_dev = activity.shape[0]
    trials = activity.shape[2]
    quarter = activity.shape[3]
    slot_cap = slot_src.shape[0]
    sub_width = weights.shape[3]
    n_parts = sub_width // quarter
    offsets = (-1, 1, n_areas // 2)

    occupied = jnp.arange(slot_cap) < slot_count[0]
    same = ((slot_dst[:, None] == slot_dst[None, :]) & occupied[None, :]).astype(jnp.float32)
    earlier = (slot_dst[:, None] == slot_dst[None, :]) & occupied[None, :] & (
        jnp.arange(slot_cap)[None, :] < jnp.arange(slot_cap)[:, None]
    )
    lead = occupied & ~jnp.any(earlier, axis=1)
    first = ((slot_dst[:, None] == jnp.arange(sub_dev)[None, :]) & lead[:, None]).astype(jnp.float32)

    wanted = jnp.clip(slot_src % sub_dev, 0, sub_dev - 1).astype(jnp.int32)
    provide = []
    for k in range(slot_cap):
        perm = [(i, (i + offsets[k]) % n_areas) for i in range(n_areas)]
        provide.append(lax.ppermute(wanted[k], "area", perm))

    w_full = lax.all_gather(weights[:, 0], "blk", axis=1, tiled=False)
    state = jnp.stack([activity[:, 0], ext_input[:, 0].astype(jnp.float32)], axis=1)
    state_full = lax.all_gather(state, "blk", axis=2, tiled=False)
    state_full = state_full.transpose(1, 0, 3, 2, 4).reshape(2, sub_dev, trials, sub_width)
    current = state_full[0]
    drive_in = state_full[1]

    def exchange(rate_full):
        got = []
        for k in range(slot_cap):
            payload = lax.dynamic_index_in_dim(rate_full, provide[k], 0, keepdims=False)
            perm = [(i, (i - offsets[k]) % n_areas) for i in range(n_areas)]
            got.append(lax.ppermute(payload, "area", perm))
        return jnp.stack(got)

    rate_full = jnp.tanh(current).astype(jnp.bfloat16)
    pre_list = []
    post_list = []
    for step_idx in range(STEPS):
        presyn = exchange(rate_full)
        presyn_parts = presyn.reshape(slot_cap, trials, n_parts, quarter)
        contrib = jnp.einsum("knjq,kjqv->kjnv", presyn_parts, w_full, preferred_element_type=jnp.float32)
        per_slot = []
        for k in range(slot_cap):
            grouped = sum(same[k, l] * contrib[l] for l in range(slot_cap))
            per_slot.append(jnp.sum(grouped.astype(jnp.bfloat16).astype(jnp.float32), axis=0))
        summed = sum(first[k][:, None, None] * per_slot[k][None] for k in range(slot_cap))
        current = current + euler_step * (summed - current + drive_in)
        rate_full = jnp.tanh(current).astype(jnp.bfloat16)
        pre_list.append(lax.dynamic_slice_in_dim(presyn, my_blk * quarter, quarter, 2))
        post_list.append(rate_full)
    final_state = lax.dynamic_slice_in_dim(current, my_blk * quarter, quarter, 2)[:, None]

    pre_centered = centre(jnp.stack(pre_list, axis=1))
    post_centered = centre(jnp.stack(post_list, axis=0))
    post_sel = jnp.take(post_centered, slot_dst, axis=1).transpose(1, 0, 2, 3)
    change = jnp.einsum("ktnq,ktnu->kqu", pre_centered, post_sel, preferred_element_type=jnp.float32)
    gate_on = (occupied & (hebb_mask == 1)).astype(jnp.float32)
    norm_scale = (STEPS * trials) ** (-0.5)
    plasticity = (change * gate_on[:, None, None] * norm_scale).astype(jnp.bfloat16)[:, None]
    return (final_state, plasticity)


def solution(mesh):
    in_specs = (
        P("area", "blk", None, None),
        P("area", "blk", None, None),
        P("area", "blk", None, None),
        P("area"),
        P("area"),
        P("area"),
        P("area"),
    )
    out_specs = (P("area", "blk", None, None), P("area", "blk", None, None))
    return jax.shard_map(body, mesh=mesh, in_specs=in_specs, out_specs=out_specs, check_vma=False)
```

```python
import jax
import jax.numpy as jnp
from jax import lax
from jax.sharding import PartitionSpec as P

STEPS = 4


euler_step = 0.5


def centre(x):
    xf = x.astype(jnp.float32)
    return (xf - jnp.mean(xf, axis=-2, keepdims=True)).astype(jnp.bfloat16)


def body(activity, ext_input, weights, slot_dst, slot_src, slot_count, hebb_mask):
    n_areas = lax.axis_size("area")
    n_blk = lax.axis_size("blk")
    my_blk = lax.axis_index("blk")
    sub_dev = activity.shape[0]
    trials = activity.shape[2]
    quarter = activity.shape[3]
    slot_cap = slot_src.shape[0]
    sub_width = weights.shape[3]
    n_parts = sub_width // quarter
    offsets = (-1, 1, n_areas // 2)

    occupied = jnp.arange(slot_cap) < slot_count[0]
    same = ((slot_dst[:, None] == slot_dst[None, :]) & occupied[None, :]).astype(jnp.float32)
    earlier = (slot_dst[:, None] == slot_dst[None, :]) & occupied[None, :] & (
        jnp.arange(slot_cap)[None, :] < jnp.arange(slot_cap)[:, None]
    )
    lead = occupied & ~jnp.any(earlier, axis=1)
    first = ((slot_dst[:, None] == jnp.arange(sub_dev)[None, :]) & lead[:, None]).astype(jnp.float32)

    wanted = jnp.clip(slot_src % sub_dev, 0, sub_dev - 1).astype(jnp.int32)
    provide = []
    for k in range(slot_cap):
        perm = [(i, (i + offsets[k]) % n_areas) for i in range(n_areas)]
        provide.append(lax.ppermute(wanted[k], "area", perm))

    w_full = lax.all_gather(weights[:, 0], "blk", axis=1, tiled=False)
    ext_full = lax.all_gather(ext_input[:, 0], "blk", axis=1, tiled=False)
    drive_in = ext_full.transpose(0, 2, 1, 3).reshape(sub_dev, trials, sub_width).astype(jnp.float32)
    own_act = activity[:, 0]
    by_shift = [own_act] + [
        lax.ppermute(own_act, "blk", [(b, (b + s) % n_blk) for b in range(n_blk)]) for s in range(1, n_blk)
    ]
    by_shift = jnp.stack(by_shift, axis=1)
    part_to_shift = (my_blk - jnp.arange(n_blk)) % n_blk
    act_full = jnp.take(by_shift, part_to_shift, axis=1)
    current = act_full.transpose(0, 2, 1, 3).reshape(sub_dev, trials, sub_width)

    def exchange(rate_full):
        got = []
        for k in range(slot_cap):
            payload = lax.dynamic_index_in_dim(rate_full, provide[k], 0, keepdims=False)
            perm = [(i, (i - offsets[k]) % n_areas) for i in range(n_areas)]
            got.append(lax.ppermute(payload, "area", perm))
        return jnp.stack(got)

    same_b = same.astype(jnp.bfloat16)
    w_rhs = w_full.transpose(1, 0, 2, 3).reshape(n_parts, slot_cap * quarter, sub_width)
    rate_full = jnp.tanh(current).astype(jnp.bfloat16)
    pre_list = []
    post_list = []
    for step_idx in range(STEPS):
        presyn = exchange(rate_full)
        presyn_parts = presyn.reshape(slot_cap, trials, n_parts, quarter)
        lhs = same_b[None, :, None, :, None] * presyn_parts.transpose(2, 1, 0, 3)[:, None]
        lhs = lhs.reshape(n_parts, slot_cap * trials, slot_cap * quarter)
        grouped = lax.dot_general(
            lhs, w_rhs, (((2,), (1,)), ((0,), (0,))), preferred_element_type=jnp.float32
        )
        per_slot = jnp.sum(grouped.astype(jnp.bfloat16).astype(jnp.float32), axis=0)
        per_slot = per_slot.reshape(slot_cap, trials, sub_width)
        summed = jnp.einsum("kd,knv->dnv", first, per_slot, precision=lax.Precision.HIGHEST)
        current = current + euler_step * (summed - current + drive_in)
        rate_full = jnp.tanh(current).astype(jnp.bfloat16)
        pre_list.append(lax.dynamic_slice_in_dim(presyn, my_blk * quarter, quarter, 2))
        post_list.append(rate_full)
    final_state = lax.dynamic_slice_in_dim(current, my_blk * quarter, quarter, 2)[:, None]

    pre_centered = centre(jnp.stack(pre_list, axis=1))
    post_centered = centre(jnp.stack(post_list, axis=0))
    post_sel = jnp.take(post_centered, slot_dst, axis=1).transpose(1, 0, 2, 3)
    change = jnp.einsum("ktnq,ktnu->kqu", pre_centered, post_sel, preferred_element_type=jnp.float32)
    gate_on = (occupied & (hebb_mask == 1)).astype(jnp.float32)
    norm_scale = (STEPS * trials) ** (-0.5)
    plasticity = (change * gate_on[:, None, None] * norm_scale).astype(jnp.bfloat16)[:, None]
    return (final_state, plasticity)


def solution(mesh):
    in_specs = (
        P("area", "blk", None, None),
        P("area", "blk", None, None),
        P("area", "blk", None, None),
        P("area"),
        P("area"),
        P("area"),
        P("area"),
    )
    out_specs = (P("area", "blk", None, None), P("area", "blk", None, None))
    return jax.shard_map(body, mesh=mesh, in_specs=in_specs, out_specs=out_specs, check_vma=False)
```

```python
import jax
import jax.numpy as jnp
from jax import lax
from jax.sharding import PartitionSpec as P

STEPS = 4


euler_step = 0.5


def centre(x):
    xf = x.astype(jnp.float32)
    return (xf - jnp.mean(xf, axis=-2, keepdims=True)).astype(jnp.bfloat16)


def body(activity, ext_input, weights, slot_dst, slot_src, slot_count, hebb_mask):
    n_areas = lax.axis_size("area")
    n_blk = lax.axis_size("blk")
    my_blk = lax.axis_index("blk")
    sub_dev = activity.shape[0]
    trials = activity.shape[2]
    quarter = activity.shape[3]
    slot_cap = slot_src.shape[0]
    sub_width = weights.shape[3]
    n_parts = sub_width // quarter
    offsets = (-1, 1, n_areas // 2)

    occupied = jnp.arange(slot_cap) < slot_count[0]
    same = ((slot_dst[:, None] == slot_dst[None, :]) & occupied[None, :]).astype(jnp.float32)
    earlier = (slot_dst[:, None] == slot_dst[None, :]) & occupied[None, :] & (
        jnp.arange(slot_cap)[None, :] < jnp.arange(slot_cap)[:, None]
    )
    lead = occupied & ~jnp.any(earlier, axis=1)
    first = ((slot_dst[:, None] == jnp.arange(sub_dev)[None, :]) & lead[:, None]).astype(jnp.float32)

    wanted = jnp.clip(slot_src % sub_dev, 0, sub_dev - 1).astype(jnp.int32)
    provide = []
    for k in range(slot_cap):
        perm = [(i, (i + offsets[k]) % n_areas) for i in range(n_areas)]
        provide.append(lax.ppermute(wanted[k], "area", perm))

    w_full = lax.all_gather(weights[:, 0], "blk", axis=1, tiled=False)
    own_state = jnp.stack([activity[:, 0], ext_input[:, 0].astype(jnp.float32)])
    by_shift = [own_state] + [
        lax.ppermute(own_state, "blk", [(b, (b + s) % n_blk) for b in range(n_blk)]) for s in range(1, n_blk)
    ]
    by_shift = jnp.stack(by_shift, axis=2)
    part_to_shift = (my_blk - jnp.arange(n_blk)) % n_blk
    state_full = jnp.take(by_shift, part_to_shift, axis=2)
    state_full = state_full.transpose(0, 1, 3, 2, 4).reshape(2, sub_dev, trials, sub_width)
    current = state_full[0]
    drive_in = state_full[1]

    def exchange(rate_full):
        got = []
        for k in range(slot_cap):
            payload = lax.dynamic_index_in_dim(rate_full, provide[k], 0, keepdims=False)
            perm = [(i, (i - offsets[k]) % n_areas) for i in range(n_areas)]
            got.append(lax.ppermute(payload, "area", perm))
        return jnp.stack(got)

    same_b = same.astype(jnp.bfloat16)
    w_rhs = w_full.transpose(1, 0, 2, 3).reshape(n_parts, slot_cap * quarter, sub_width)
    rate_full = jnp.tanh(current).astype(jnp.bfloat16)
    pre_list = []
    post_list = []
    for step_idx in range(STEPS):
        presyn = exchange(rate_full)
        presyn_parts = presyn.reshape(slot_cap, trials, n_parts, quarter)
        lhs = same_b[None, :, None, :, None] * presyn_parts.transpose(2, 1, 0, 3)[:, None]
        lhs = lhs.reshape(n_parts, slot_cap * trials, slot_cap * quarter)
        grouped = lax.dot_general(
            lhs, w_rhs, (((2,), (1,)), ((0,), (0,))), preferred_element_type=jnp.float32
        )
        per_slot = jnp.sum(grouped.astype(jnp.bfloat16).astype(jnp.float32), axis=0)
        per_slot = per_slot.reshape(slot_cap, trials, sub_width)
        summed = jnp.einsum("kd,knv->dnv", first, per_slot, precision=lax.Precision.HIGHEST)
        current = current + euler_step * (summed - current + drive_in)
        rate_full = jnp.tanh(current).astype(jnp.bfloat16)
        pre_list.append(lax.dynamic_slice_in_dim(presyn, my_blk * quarter, quarter, 2))
        post_list.append(rate_full)
    final_state = lax.dynamic_slice_in_dim(current, my_blk * quarter, quarter, 2)[:, None]

    pre_centered = centre(jnp.stack(pre_list, axis=1))
    post_centered = centre(jnp.stack(post_list, axis=0))
    post_sel = jnp.take(post_centered, slot_dst, axis=1).transpose(1, 0, 2, 3)
    change = jnp.einsum("ktnq,ktnu->kqu", pre_centered, post_sel, preferred_element_type=jnp.float32)
    gate_on = (occupied & (hebb_mask == 1)).astype(jnp.float32)
    norm_scale = (STEPS * trials) ** (-0.5)
    plasticity = (change * gate_on[:, None, None] * norm_scale).astype(jnp.bfloat16)[:, None]
    return (final_state, plasticity)


def solution(mesh):
    in_specs = (
        P("area", "blk", None, None),
        P("area", "blk", None, None),
        P("area", "blk", None, None),
        P("area"),
        P("area"),
        P("area"),
        P("area"),
    )
    out_specs = (P("area", "blk", None, None), P("area", "blk", None, None))
    return jax.shard_map(body, mesh=mesh, in_specs=in_specs, out_specs=out_specs, check_vma=False)
```

```python
import jax
import jax.numpy as jnp
from jax import lax
from jax.sharding import PartitionSpec as P

STEPS = 4


euler_step = 0.5


def centre(x):
    xf = x.astype(jnp.float32)
    return (xf - jnp.mean(xf, axis=-2, keepdims=True)).astype(jnp.bfloat16)


def body(activity, ext_input, weights, slot_dst, slot_src, slot_count, hebb_mask):
    n_areas = lax.axis_size("area")
    n_blk = lax.axis_size("blk")
    my_blk = lax.axis_index("blk")
    sub_dev = activity.shape[0]
    trials = activity.shape[2]
    quarter = activity.shape[3]
    slot_cap = slot_src.shape[0]
    sub_width = weights.shape[3]
    offsets = (-1, 1, n_areas // 2)

    occupied = jnp.arange(slot_cap) < slot_count[0]
    select = ((slot_dst[:, None] == jnp.arange(sub_dev)[None, :]) & occupied[:, None]).astype(jnp.float32)

    wanted = jnp.clip(slot_src % sub_dev, 0, sub_dev - 1).astype(jnp.int32)
    provide = []
    for k in range(slot_cap):
        perm = [(i, (i + offsets[k]) % n_areas) for i in range(n_areas)]
        provide.append(lax.ppermute(wanted[k], "area", perm))
    provide = jnp.stack(provide)
    select_provided = jnp.take(select, provide, axis=1)

    w_full = lax.all_gather(weights[:, 0], "blk", axis=1, tiled=False)
    w_full = w_full.reshape(slot_cap, sub_width, sub_width)
    own_state = jnp.stack([activity[:, 0], ext_input[:, 0].astype(jnp.float32)])
    by_shift = [own_state] + [
        lax.ppermute(own_state, "blk", [(b, (b + s) % n_blk) for b in range(n_blk)]) for s in range(1, n_blk)
    ]
    by_shift = jnp.stack(by_shift, axis=2)
    part_to_shift = (my_blk - jnp.arange(n_blk)) % n_blk
    state_full = jnp.take(by_shift, part_to_shift, axis=2)
    state_full = state_full.transpose(0, 1, 3, 2, 4).reshape(2, sub_dev, trials, sub_width)
    current = state_full[0]
    drive_in = state_full[1]
    drive_provided = jnp.take(drive_in, provide, axis=0)

    def advance(cur, contrib, sel, drive):
        summed = sum(sel[k][:, None, None] * contrib[k][None] for k in range(slot_cap))
        return cur + euler_step * (summed - cur + drive)

    def exchange(payload):
        got = []
        for k in range(slot_cap):
            perm = [(i, (i - offsets[k]) % n_areas) for i in range(n_areas)]
            got.append(lax.ppermute(payload[k], "area", perm))
        return jnp.stack(got)

    payload = jnp.tanh(jnp.take(current, provide, axis=0)).astype(jnp.bfloat16)
    pre_list = []
    post_list = []
    for step_idx in range(STEPS):
        presyn = exchange(payload)
        contrib = jnp.einsum("knu,kuv->knv", presyn, w_full, preferred_element_type=jnp.float32)
        if step_idx + 1 < STEPS:
            provided_now = advance(jnp.take(current, provide, axis=0), contrib, select_provided, drive_provided)
            payload = jnp.tanh(provided_now).astype(jnp.bfloat16)
        current = advance(current, contrib, select, drive_in)
        pre_list.append(lax.dynamic_slice_in_dim(presyn, my_blk * quarter, quarter, 2))
        post_list.append(jnp.tanh(jnp.take(current, slot_dst, axis=0)).astype(jnp.bfloat16))
    final_state = lax.dynamic_slice_in_dim(current, my_blk * quarter, quarter, 2)[:, None]

    pre_centered = centre(jnp.stack(pre_list, axis=1))
    post_centered = centre(jnp.stack(post_list, axis=1))
    change = jnp.einsum("ktnq,ktnu->kqu", pre_centered, post_centered, preferred_element_type=jnp.float32)
    gate_on = (occupied & (hebb_mask == 1)).astype(jnp.float32)
    norm_scale = (STEPS * trials) ** (-0.5)
    plasticity = (change * gate_on[:, None, None] * norm_scale).astype(jnp.bfloat16)[:, None]
    return (final_state, plasticity)


def solution(mesh):
    in_specs = (
        P("area", "blk", None, None),
        P("area", "blk", None, None),
        P("area", "blk", None, None),
        P("area"),
        P("area"),
        P("area"),
        P("area"),
    )
    out_specs = (P("area", "blk", None, None), P("area", "blk", None, None))
    return jax.shard_map(body, mesh=mesh, in_specs=in_specs, out_specs=out_specs, check_vma=False)
```

```python
import jax
import jax.numpy as jnp
from jax import lax
from jax.sharding import PartitionSpec as P

STEPS = 4


euler_step = 0.5


def centre(x):
    xf = x.astype(jnp.float32)
    return (xf - jnp.mean(xf, axis=-2, keepdims=True)).astype(jnp.bfloat16)


def body(activity, ext_input, weights, slot_dst, slot_src, slot_count, hebb_mask):
    n_areas = lax.axis_size("area")
    n_blk = lax.axis_size("blk")
    my_blk = lax.axis_index("blk")
    sub_dev = activity.shape[0]
    trials = activity.shape[2]
    quarter = activity.shape[3]
    slot_cap = slot_src.shape[0]
    sub_width = weights.shape[3]
    offsets = (-1, 1, n_areas // 2)

    occupied = jnp.arange(slot_cap) < slot_count[0]
    select = ((slot_dst[:, None] == jnp.arange(sub_dev)[None, :]) & occupied[:, None]).astype(jnp.float32)

    wanted = jnp.clip(slot_src % sub_dev, 0, sub_dev - 1).astype(jnp.int32)
    provide = []
    for k in range(slot_cap):
        perm = [(i, (i + offsets[k]) % n_areas) for i in range(n_areas)]
        provide.append(lax.ppermute(wanted[k], "area", perm))
    provide = jnp.stack(provide)
    select_provided = jnp.take(select, provide, axis=1)

    w_full = lax.all_gather(weights[:, 0], "blk", axis=1, tiled=False)
    w_full = w_full.reshape(slot_cap, sub_width, sub_width)
    own_state = jnp.stack([activity[:, 0], ext_input[:, 0].astype(jnp.float32)])
    by_shift = [own_state] + [
        lax.ppermute(own_state, "blk", [((b + s) % n_blk, b) for b in range(n_blk)]) for s in range(1, n_blk)
    ]
    twice = jnp.stack(by_shift + by_shift, axis=2)
    state_full = lax.dynamic_slice_in_dim(twice, (n_blk - my_blk) % n_blk, n_blk, axis=2)
    state_full = state_full.transpose(0, 1, 3, 2, 4).reshape(2, sub_dev, trials, sub_width)
    current = state_full[0]
    drive_in = state_full[1]

    def pick(x, idx):
        return jnp.stack([lax.dynamic_index_in_dim(x, idx[k], 0, keepdims=False) for k in range(slot_cap)])

    drive_provided = pick(drive_in, provide)

    def advance(cur, contrib, sel, drive):
        summed = sum(sel[k][:, None, None] * contrib[k][None] for k in range(slot_cap))
        return cur + euler_step * (summed - cur + drive)

    def exchange(payload):
        got = []
        for k in range(slot_cap):
            perm = [(i, (i - offsets[k]) % n_areas) for i in range(n_areas)]
            got.append(lax.ppermute(payload[k], "area", perm))
        return jnp.stack(got)

    payload = jnp.tanh(pick(current, provide)).astype(jnp.bfloat16)
    pre_list = []
    post_list = []
    for step_idx in range(STEPS):
        presyn = exchange(payload)
        contrib = jnp.einsum("knu,kuv->knv", presyn, w_full, preferred_element_type=jnp.float32)
        if step_idx + 1 < STEPS:
            provided_now = advance(pick(current, provide), contrib, select_provided, drive_provided)
            payload = jnp.tanh(provided_now).astype(jnp.bfloat16)
        current = advance(current, contrib, select, drive_in)
        pre_list.append(lax.dynamic_slice_in_dim(presyn, my_blk * quarter, quarter, 2))
        post_list.append(jnp.tanh(pick(current, slot_dst)).astype(jnp.bfloat16))
    final_state = lax.dynamic_slice_in_dim(current, my_blk * quarter, quarter, 2)[:, None]

    pre_centered = centre(jnp.stack(pre_list, axis=1))
    post_centered = centre(jnp.stack(post_list, axis=1))
    change = jnp.einsum("ktnq,ktnu->kqu", pre_centered, post_centered, preferred_element_type=jnp.float32)
    gate_on = (occupied & (hebb_mask == 1)).astype(jnp.float32)
    norm_scale = (STEPS * trials) ** (-0.5)
    plasticity = (change * gate_on[:, None, None] * norm_scale).astype(jnp.bfloat16)[:, None]
    return (final_state, plasticity)


def solution(mesh):
    in_specs = (
        P("area", "blk", None, None),
        P("area", "blk", None, None),
        P("area", "blk", None, None),
        P("area"),
        P("area"),
        P("area"),
        P("area"),
    )
    out_specs = (P("area", "blk", None, None), P("area", "blk", None, None))
    return jax.shard_map(body, mesh=mesh, in_specs=in_specs, out_specs=out_specs, check_vma=False)
```

```python
import jax
import jax.numpy as jnp
from jax import lax
from jax.sharding import PartitionSpec as P

STEPS = 4


euler_step = 0.5


def centre(x):
    xf = x.astype(jnp.float32)
    return (xf - jnp.mean(xf, axis=-2, keepdims=True)).astype(jnp.bfloat16)


def body(activity, ext_input, weights, slot_dst, slot_src, slot_count, hebb_mask):
    n_areas = lax.axis_size("area")
    n_blk = lax.axis_size("blk")
    my_blk = lax.axis_index("blk")
    sub_dev = activity.shape[0]
    trials = activity.shape[2]
    quarter = activity.shape[3]
    slot_cap = slot_src.shape[0]
    sub_width = weights.shape[3]
    offsets = (-1, 1, n_areas // 2)

    occupied = jnp.arange(slot_cap) < slot_count[0]
    select = ((slot_dst[:, None] == jnp.arange(sub_dev)[None, :]) & occupied[:, None]).astype(jnp.float32)

    wanted = jnp.clip(slot_src % sub_dev, 0, sub_dev - 1).astype(jnp.int32)
    provide = []
    for k in range(slot_cap):
        perm = [(i, (i + offsets[k]) % n_areas) for i in range(n_areas)]
        provide.append(lax.ppermute(wanted[k], "area", perm))
    provide = jnp.stack(provide)
    select_provided = jnp.take(select, provide, axis=1)

    w_full = lax.all_gather(weights[:, 0], "blk", axis=1, tiled=False)
    w_full = w_full.reshape(slot_cap, sub_width, sub_width)
    own_state = jnp.stack([activity[:, 0], ext_input[:, 0].astype(jnp.float32)])
    by_shift = [own_state] + [
        lax.ppermute(own_state, "blk", [((b + s) % n_blk, b) for b in range(n_blk)]) for s in range(1, n_blk)
    ]

    def in_part_order(pieces):
        ordered = []
        for j in range(n_blk):
            shift_j = (j - my_blk) % n_blk
            out = pieces[0]
            for s in range(1, n_blk):
                out = jnp.where(shift_j == s, pieces[s], out)
            ordered.append(out)
        return jnp.stack(ordered, axis=-2)

    def pick(x, idx):
        return jnp.stack([lax.dynamic_index_in_dim(x, idx[k], 0, keepdims=False) for k in range(slot_cap)])

    state_full = in_part_order(by_shift).reshape(2, sub_dev, trials, sub_width)
    current = state_full[0]
    drive_in = state_full[1]
    drive_provided = pick(drive_in, provide)
    first_act = in_part_order([pick(piece[0], provide) for piece in by_shift]).reshape(slot_cap, trials, sub_width)

    def advance(cur, contrib, sel, drive):
        summed = sum(sel[k][:, None, None] * contrib[k][None] for k in range(slot_cap))
        return cur + euler_step * (summed - cur + drive)

    def exchange(payload):
        got = []
        for k in range(slot_cap):
            perm = [(i, (i - offsets[k]) % n_areas) for i in range(n_areas)]
            got.append(lax.ppermute(payload[k], "area", perm))
        return jnp.stack(got)

    payload = jnp.tanh(first_act).astype(jnp.bfloat16)
    pre_list = []
    post_list = []
    for step_idx in range(STEPS):
        presyn = exchange(payload)
        contrib = jnp.einsum("knu,kuv->knv", presyn, w_full, preferred_element_type=jnp.float32)
        if step_idx + 1 < STEPS:
            provided_now = advance(pick(current, provide), contrib, select_provided, drive_provided)
            payload = jnp.tanh(provided_now).astype(jnp.bfloat16)
        current = advance(current, contrib, select, drive_in)
        pre_list.append(lax.dynamic_slice_in_dim(presyn, my_blk * quarter, quarter, 2))
        post_list.append(jnp.tanh(pick(current, slot_dst)).astype(jnp.bfloat16))
    final_state = lax.dynamic_slice_in_dim(current, my_blk * quarter, quarter, 2)[:, None]

    pre_centered = centre(jnp.stack(pre_list, axis=1))
    post_centered = centre(jnp.stack(post_list, axis=1))
    change = jnp.einsum("ktnq,ktnu->kqu", pre_centered, post_centered, preferred_element_type=jnp.float32)
    gate_on = (occupied & (hebb_mask == 1)).astype(jnp.float32)
    norm_scale = (STEPS * trials) ** (-0.5)
    plasticity = (change * gate_on[:, None, None] * norm_scale).astype(jnp.bfloat16)[:, None]
    return (final_state, plasticity)


def solution(mesh):
    in_specs = (
        P("area", "blk", None, None),
        P("area", "blk", None, None),
        P("area", "blk", None, None),
        P("area"),
        P("area"),
        P("area"),
        P("area"),
    )
    out_specs = (P("area", "blk", None, None), P("area", "blk", None, None))
    return jax.shard_map(body, mesh=mesh, in_specs=in_specs, out_specs=out_specs, check_vma=False)
```

```python
import jax
import jax.numpy as jnp
from jax import lax
from jax.sharding import PartitionSpec as P

STEPS = 4


euler_step = 0.5


def centre(x):
    xf = x.astype(jnp.float32)
    return (xf - jnp.mean(xf, axis=-2, keepdims=True)).astype(jnp.bfloat16)


def body(activity, ext_input, weights, slot_dst, slot_src, slot_count, hebb_mask):
    n_areas = lax.axis_size("area")
    n_blk = lax.axis_size("blk")
    my_blk = lax.axis_index("blk")
    sub_dev = activity.shape[0]
    trials = activity.shape[2]
    quarter = activity.shape[3]
    slot_cap = slot_src.shape[0]
    sub_width = weights.shape[3]
    offsets = (-1, 1, n_areas // 2)

    occupied = jnp.arange(slot_cap) < slot_count[0]
    select = ((slot_dst[:, None] == jnp.arange(sub_dev)[None, :]) & occupied[:, None]).astype(jnp.float32)

    wanted = jnp.clip(slot_src % sub_dev, 0, sub_dev - 1).astype(jnp.int32)
    provide = []
    for k in range(slot_cap):
        perm = [(i, (i + offsets[k]) % n_areas) for i in range(n_areas)]
        provide.append(lax.ppermute(wanted[k], "area", perm))
    provide = jnp.stack(provide)
    select_provided = ((slot_dst[:, None] == provide[None, :]) & occupied[:, None]).astype(jnp.float32)

    own_state = jnp.stack([activity[:, 0], ext_input[:, 0].astype(jnp.float32)])
    by_shift = [own_state] + [
        lax.ppermute(own_state, "blk", [((b + s) % n_blk, b) for b in range(n_blk)]) for s in range(1, n_blk)
    ]

    def in_part_order(pieces, axis=-2):
        ordered = []
        for j in range(n_blk):
            shift_j = (j - my_blk) % n_blk
            out = pieces[0]
            for s in range(1, n_blk):
                out = jnp.where(shift_j == s, pieces[s], out)
            ordered.append(out)
        return jnp.stack(ordered, axis=axis)

    own_w = weights[:, 0]
    w_pieces = [own_w] + [
        lax.ppermute(own_w, "blk", [((b + s) % n_blk, b) for b in range(n_blk)]) for s in range(1, n_blk)
    ]
    w_full = in_part_order(w_pieces, axis=1).reshape(slot_cap, sub_width, sub_width)

    def pick(x, idx):
        return jnp.stack([lax.dynamic_index_in_dim(x, idx[k], 0, keepdims=False) for k in range(slot_cap)])

    state_full = in_part_order(by_shift).reshape(2, sub_dev, trials, sub_width)
    current = state_full[0]
    drive_in = state_full[1]
    drive_provided = pick(drive_in, provide)
    first_act = in_part_order([pick(piece[0], provide) for piece in by_shift]).reshape(slot_cap, trials, sub_width)

    def advance(cur, contrib, sel, drive):
        summed = sum(sel[k][:, None, None] * contrib[k][None] for k in range(slot_cap))
        return cur + euler_step * (summed - cur + drive)

    def exchange(payload):
        got = []
        for k in range(slot_cap):
            perm = [(i, (i - offsets[k]) % n_areas) for i in range(n_areas)]
            got.append(lax.ppermute(payload[k], "area", perm))
        return jnp.stack(got)

    payload = jnp.tanh(first_act).astype(jnp.bfloat16)
    pre_list = []
    post_list = []
    for step_idx in range(STEPS):
        presyn = exchange(payload)
        contrib = jnp.einsum("knu,kuv->knv", presyn, w_full, preferred_element_type=jnp.float32)
        if step_idx + 1 < STEPS:
            provided_now = advance(pick(current, provide), contrib, select_provided, drive_provided)
            payload = jnp.tanh(provided_now).astype(jnp.bfloat16)
        current = advance(current, contrib, select, drive_in)
        pre_list.append(lax.dynamic_slice_in_dim(presyn, my_blk * quarter, quarter, 2))
        post_list.append(jnp.tanh(pick(current, slot_dst)).astype(jnp.bfloat16))
    final_state = lax.dynamic_slice_in_dim(current, my_blk * quarter, quarter, 2)[:, None]

    pre_centered = centre(jnp.stack(pre_list, axis=1))
    post_centered = centre(jnp.stack(post_list, axis=1))
    change = jnp.einsum("ktnq,ktnu->kqu", pre_centered, post_centered, preferred_element_type=jnp.float32)
    gate_on = (occupied & (hebb_mask == 1)).astype(jnp.float32)
    norm_scale = (STEPS * trials) ** (-0.5)
    plasticity = (change * gate_on[:, None, None] * norm_scale).astype(jnp.bfloat16)[:, None]
    return (final_state, plasticity)


def solution(mesh):
    in_specs = (
        P("area", "blk", None, None),
        P("area", "blk", None, None),
        P("area", "blk", None, None),
        P("area"),
        P("area"),
        P("area"),
        P("area"),
    )
    out_specs = (P("area", "blk", None, None), P("area", "blk", None, None))
    return jax.shard_map(body, mesh=mesh, in_specs=in_specs, out_specs=out_specs, check_vma=False)
```

```python
import jax
import jax.numpy as jnp
from jax import lax
from jax.sharding import PartitionSpec as P

STEPS = 4


euler_step = 0.5


def centre(x):
    xf = x.astype(jnp.float32)
    return (xf - jnp.mean(xf, axis=-2, keepdims=True)).astype(jnp.bfloat16)


def body(activity, ext_input, weights, slot_dst, slot_src, slot_count, hebb_mask):
    n_areas = lax.axis_size("area")
    n_blk = lax.axis_size("blk")
    my_blk = lax.axis_index("blk")
    sub_dev = activity.shape[0]
    trials = activity.shape[2]
    quarter = activity.shape[3]
    slot_cap = slot_src.shape[0]
    sub_width = weights.shape[3]
    offsets = (-1, 1, n_areas // 2)

    occupied = jnp.arange(slot_cap) < slot_count[0]
    select = ((slot_dst[:, None] == jnp.arange(sub_dev)[None, :]) & occupied[:, None]).astype(jnp.float32)

    wanted = jnp.clip(slot_src % sub_dev, 0, sub_dev - 1).astype(jnp.int32)
    provide = []
    for k in range(slot_cap):
        perm = [(i, (i + offsets[k]) % n_areas) for i in range(n_areas)]
        provide.append(lax.ppermute(wanted[k], "area", perm))
    provide = jnp.stack(provide)
    select_provided = ((slot_dst[:, None] == provide[None, :]) & occupied[:, None]).astype(jnp.float32)

    own_state = jnp.stack([activity[:, 0], ext_input[:, 0].astype(jnp.float32)])
    by_shift = [own_state] + [
        lax.ppermute(own_state, "blk", [((b + s) % n_blk, b) for b in range(n_blk)]) for s in range(1, n_blk)
    ]

    def in_part_order(pieces, axis=-2):
        ordered = []
        for j in range(n_blk):
            shift_j = (j - my_blk) % n_blk
            out = pieces[0]
            for s in range(1, n_blk):
                out = jnp.where(shift_j == s, pieces[s], out)
            ordered.append(out)
        return jnp.stack(ordered, axis=axis)


    def pick(x, idx):
        return jnp.stack([lax.dynamic_index_in_dim(x, idx[k], 0, keepdims=False) for k in range(slot_cap)])

    state_full = in_part_order(by_shift).reshape(2, sub_dev, trials, sub_width)
    current = state_full[0]
    drive_in = state_full[1]
    drive_provided = pick(drive_in, provide)
    first_act = in_part_order([pick(piece[0], provide) for piece in by_shift]).reshape(slot_cap, trials, sub_width)

    def advance(cur, contrib, sel, drive):
        summed = sum(sel[k][:, None, None] * contrib[k][None] for k in range(slot_cap))
        return cur + euler_step * (summed - cur + drive)

    def exchange(payload):
        got = []
        for k in range(slot_cap):
            perm = [(i, (i - offsets[k]) % n_areas) for i in range(n_areas)]
            got.append(lax.ppermute(payload[k], "area", perm))
        return jnp.stack(got)

    payload = jnp.tanh(first_act).astype(jnp.bfloat16)
    own_w, payload = lax.optimization_barrier((weights[:, 0], payload))
    w_pieces = [own_w] + [
        lax.ppermute(own_w, "blk", [((b + s) % n_blk, b) for b in range(n_blk)]) for s in range(1, n_blk)
    ]
    w_full = in_part_order(w_pieces, axis=1).reshape(slot_cap, sub_width, sub_width)
    pre_list = []
    post_list = []
    for step_idx in range(STEPS):
        presyn = exchange(payload)
        contrib = jnp.einsum("knu,kuv->knv", presyn, w_full, preferred_element_type=jnp.float32)
        if step_idx + 1 < STEPS:
            provided_now = advance(pick(current, provide), contrib, select_provided, drive_provided)
            payload = jnp.tanh(provided_now).astype(jnp.bfloat16)
        current = advance(current, contrib, select, drive_in)
        pre_list.append(lax.dynamic_slice_in_dim(presyn, my_blk * quarter, quarter, 2))
        post_list.append(jnp.tanh(pick(current, slot_dst)).astype(jnp.bfloat16))
    final_state = lax.dynamic_slice_in_dim(current, my_blk * quarter, quarter, 2)[:, None]

    pre_centered = centre(jnp.stack(pre_list, axis=1))
    post_centered = centre(jnp.stack(post_list, axis=1))
    change = jnp.einsum("ktnq,ktnu->kqu", pre_centered, post_centered, preferred_element_type=jnp.float32)
    gate_on = (occupied & (hebb_mask == 1)).astype(jnp.float32)
    norm_scale = (STEPS * trials) ** (-0.5)
    plasticity = (change * gate_on[:, None, None] * norm_scale).astype(jnp.bfloat16)[:, None]
    return (final_state, plasticity)


def solution(mesh):
    in_specs = (
        P("area", "blk", None, None),
        P("area", "blk", None, None),
        P("area", "blk", None, None),
        P("area"),
        P("area"),
        P("area"),
        P("area"),
    )
    out_specs = (P("area", "blk", None, None), P("area", "blk", None, None))
    return jax.shard_map(body, mesh=mesh, in_specs=in_specs, out_specs=out_specs, check_vma=False)
```

```python
import jax
import jax.numpy as jnp
from jax import lax
from jax.sharding import PartitionSpec as P

STEPS = 4


euler_step = 0.5


def centre(x):
    xf = x.astype(jnp.float32)
    return (xf - jnp.mean(xf, axis=-2, keepdims=True)).astype(jnp.bfloat16)


def body(activity, ext_input, weights, slot_dst, slot_src, slot_count, hebb_mask):
    n_areas = lax.axis_size("area")
    n_blk = lax.axis_size("blk")
    my_blk = lax.axis_index("blk")
    sub_dev = activity.shape[0]
    trials = activity.shape[2]
    quarter = activity.shape[3]
    slot_cap = slot_src.shape[0]
    sub_width = weights.shape[3]
    offsets = (-1, 1, n_areas // 2)

    occupied = jnp.arange(slot_cap) < slot_count[0]
    select = ((slot_dst[:, None] == jnp.arange(sub_dev)[None, :]) & occupied[:, None]).astype(jnp.float32)

    wanted = jnp.clip(slot_src % sub_dev, 0, sub_dev - 1).astype(jnp.int32)
    provide = []
    for k in range(slot_cap):
        perm = [(i, (i + offsets[k]) % n_areas) for i in range(n_areas)]
        provide.append(lax.ppermute(wanted[k], "area", perm))
    provide = jnp.stack(provide)
    select_provided = ((slot_dst[:, None] == provide[None, :]) & occupied[:, None]).astype(jnp.float32)

    own_state = jnp.stack([activity[:, 0], ext_input[:, 0].astype(jnp.float32)])
    by_shift = [own_state] + [
        lax.ppermute(own_state, "blk", [((b + s) % n_blk, b) for b in range(n_blk)]) for s in range(1, n_blk)
    ]

    def in_part_order(pieces, axis=-2):
        ordered = []
        for j in range(n_blk):
            shift_j = (j - my_blk) % n_blk
            out = pieces[0]
            for s in range(1, n_blk):
                out = jnp.where(shift_j == s, pieces[s], out)
            ordered.append(out)
        return jnp.stack(ordered, axis=axis)


    def pick(x, idx):
        return jnp.stack([lax.dynamic_index_in_dim(x, idx[k], 0, keepdims=False) for k in range(slot_cap)])

    provide_hot = provide[:, None] == jnp.arange(sub_dev)[None, :]

    def pick_hot(x):
        return jnp.sum(jnp.where(provide_hot[:, :, None, None], x[None], jnp.zeros((), x.dtype)), axis=1)

    state_full = in_part_order(by_shift).reshape(2, sub_dev, trials, sub_width)
    current = state_full[0]
    drive_in = state_full[1]
    drive_provided = pick(drive_in, provide)
    first_act = in_part_order([pick_hot(piece[0]) for piece in by_shift]).reshape(slot_cap, trials, sub_width)

    def advance(cur, contrib, sel, drive):
        summed = sum(sel[k][:, None, None] * contrib[k][None] for k in range(slot_cap))
        return cur + euler_step * (summed - cur + drive)

    def exchange(payload):
        got = []
        for k in range(slot_cap):
            perm = [(i, (i - offsets[k]) % n_areas) for i in range(n_areas)]
            got.append(lax.ppermute(payload[k], "area", perm))
        return jnp.stack(got)

    payload = jnp.tanh(first_act).astype(jnp.bfloat16)
    own_w, payload = lax.optimization_barrier((weights[:, 0], payload))
    w_pieces = [own_w] + [
        lax.ppermute(own_w, "blk", [((b + s) % n_blk, b) for b in range(n_blk)]) for s in range(1, n_blk)
    ]
    w_full = in_part_order(w_pieces, axis=1).reshape(slot_cap, sub_width, sub_width)
    pre_list = []
    post_list = []
    for step_idx in range(STEPS):
        presyn = exchange(payload)
        contrib = jnp.einsum("knu,kuv->knv", presyn, w_full, preferred_element_type=jnp.float32)
        if step_idx + 1 < STEPS:
            provided_now = advance(pick(current, provide), contrib, select_provided, drive_provided)
            payload = jnp.tanh(provided_now).astype(jnp.bfloat16)
        current = advance(current, contrib, select, drive_in)
        pre_list.append(lax.dynamic_slice_in_dim(presyn, my_blk * quarter, quarter, 2))
        post_list.append(jnp.tanh(pick(current, slot_dst)).astype(jnp.bfloat16))
    final_state = lax.dynamic_slice_in_dim(current, my_blk * quarter, quarter, 2)[:, None]

    pre_centered = centre(jnp.stack(pre_list, axis=1))
    post_centered = centre(jnp.stack(post_list, axis=1))
    change = jnp.einsum("ktnq,ktnu->kqu", pre_centered, post_centered, preferred_element_type=jnp.float32)
    gate_on = (occupied & (hebb_mask == 1)).astype(jnp.float32)
    norm_scale = (STEPS * trials) ** (-0.5)
    plasticity = (change * gate_on[:, None, None] * norm_scale).astype(jnp.bfloat16)[:, None]
    return (final_state, plasticity)


def solution(mesh):
    in_specs = (
        P("area", "blk", None, None),
        P("area", "blk", None, None),
        P("area", "blk", None, None),
        P("area"),
        P("area"),
        P("area"),
        P("area"),
    )
    out_specs = (P("area", "blk", None, None), P("area", "blk", None, None))
    return jax.shard_map(body, mesh=mesh, in_specs=in_specs, out_specs=out_specs, check_vma=False)
```

```python
import jax
import jax.numpy as jnp
from jax import lax
from jax.sharding import PartitionSpec as P


STEPS = 4


euler_step = 0.5


def centre(x):
    xf = x.astype(jnp.float32)
    return (xf - jnp.mean(xf, axis=-2, keepdims=True)).astype(jnp.bfloat16)


def step_body(activity, ext_input, weights, slot_dst, slot_src, slot_count, hebb_mask):
    n_areas = lax.axis_size("area")
    n_blk = lax.axis_size("blk")
    my_blk = lax.axis_index("blk")
    sub_dev = activity.shape[0]
    trials = activity.shape[2]
    quarter = activity.shape[3]
    slot_cap = slot_src.shape[0]
    sub_width = weights.shape[3]
    offsets = (-1, 1, n_areas // 2)

    occupied = jnp.arange(slot_cap) < slot_count[0]
    select = ((slot_dst[:, None] == jnp.arange(sub_dev)[None, :]) & occupied[:, None]).astype(jnp.float32)

    wanted = jnp.clip(slot_src % sub_dev, 0, sub_dev - 1).astype(jnp.int32)
    provide = []
    for k in range(slot_cap):
        perm = [(i, (i + offsets[k]) % n_areas) for i in range(n_areas)]
        provide.append(lax.ppermute(wanted[k], "area", perm))
    provide = jnp.stack(provide)
    select_provided = ((slot_dst[:, None] == provide[None, :]) & occupied[:, None]).astype(jnp.float32)

    own_w = weights[:, 0]
    w_pieces = [own_w] + [
        lax.ppermute(own_w, "blk", [((b + s) % n_blk, b) for b in range(n_blk)]) for s in range(1, n_blk)
    ]
    own_state = activity[:, 0]
    by_shift = [own_state] + [
        lax.ppermute(own_state, "blk", [((b + s) % n_blk, b) for b in range(n_blk)]) for s in range(1, n_blk)
    ]

    def in_part_order(pieces, axis=-2):
        ordered = []
        for j in range(n_blk):
            shift_j = (j - my_blk) % n_blk
            out = pieces[0]
            for s in range(1, n_blk):
                out = jnp.where(shift_j == s, pieces[s], out)
            ordered.append(out)
        return jnp.stack(ordered, axis=axis)


    def pick(x, idx):
        return jnp.stack([lax.dynamic_index_in_dim(x, idx[k], 0, keepdims=False) for k in range(slot_cap)])

    provide_hot = provide[:, None] == jnp.arange(sub_dev)[None, :]

    def pick_hot(x):
        return jnp.sum(jnp.where(provide_hot[:, :, None, None], x[None], jnp.zeros((), x.dtype)), axis=1)

    w_full = in_part_order(w_pieces, axis=1).reshape(slot_cap, sub_width, sub_width)
    current = in_part_order(by_shift).reshape(sub_dev, trials, sub_width)
    first_act = in_part_order([pick_hot(piece) for piece in by_shift]).reshape(slot_cap, trials, sub_width)

    def advance(cur, contrib, sel, drive):
        summed = sum(sel[k][:, None, None] * contrib[k][None] for k in range(slot_cap))
        return cur + euler_step * (summed - cur + drive)

    def exchange(payload):
        got = []
        for k in range(slot_cap):
            perm = [(i, (i - offsets[k]) % n_areas) for i in range(n_areas)]
            got.append(lax.ppermute(payload[k], "area", perm))
        return jnp.stack(got)

    payload = jnp.tanh(first_act).astype(jnp.bfloat16)
    own_ext, payload = lax.optimization_barrier((ext_input[:, 0], payload))
    ext_pieces = [own_ext] + [
        lax.ppermute(own_ext, "blk", [((b + s) % n_blk, b) for b in range(n_blk)]) for s in range(1, n_blk)
    ]
    drive_in = in_part_order(ext_pieces).reshape(sub_dev, trials, sub_width).astype(jnp.float32)
    drive_provided = pick(drive_in, provide)
    pre_list = []
    post_list = []
    for step_idx in range(STEPS):
        presyn = exchange(payload)
        contrib = jnp.einsum("knu,kuv->knv", presyn, w_full, preferred_element_type=jnp.float32)
        if step_idx + 1 < STEPS:
            provided_now = advance(pick(current, provide), contrib, select_provided, drive_provided)
            payload = jnp.tanh(provided_now).astype(jnp.bfloat16)
        current = advance(current, contrib, select, drive_in)
        pre_list.append(lax.dynamic_slice_in_dim(presyn, my_blk * quarter, quarter, 2))
        post_list.append(jnp.tanh(pick(current, slot_dst)).astype(jnp.bfloat16))
    final_state = lax.dynamic_slice_in_dim(current, my_blk * quarter, quarter, 2)[:, None]

    pre_centered = centre(jnp.stack(pre_list, axis=1))
    post_centered = centre(jnp.stack(post_list, axis=1))
    change = jnp.einsum("ktnq,ktnu->kqu", pre_centered, post_centered, preferred_element_type=jnp.float32)
    gate_on = (occupied & (hebb_mask == 1)).astype(jnp.float32)
    norm_scale = (STEPS * trials) ** (-0.5)
    plasticity = (change * gate_on[:, None, None] * norm_scale).astype(jnp.bfloat16)[:, None]
    return (final_state, plasticity)


def solution(mesh):
    in_specs = (
        P("area", "blk", None, None),
        P("area", "blk", None, None),
        P("area", "blk", None, None),
        P("area"),
        P("area"),
        P("area"),
        P("area"),
    )
    out_specs = (P("area", "blk", None, None), P("area", "blk", None, None))
    return jax.shard_map(step_body, mesh=mesh, in_specs=in_specs, out_specs=out_specs, check_vma=False)
```

```python
import jax
import jax.numpy as jnp
from jax import lax
from jax.sharding import PartitionSpec as P

STEPS = 4


euler_step = 0.5


def centre(x):
    xf = x.astype(jnp.float32)
    return (xf - jnp.mean(xf, axis=-2, keepdims=True)).astype(jnp.bfloat16)


def body(activity, ext_input, weights, slot_dst, slot_src, slot_count, hebb_mask):
    n_areas = lax.axis_size("area")
    n_blk = lax.axis_size("blk")
    my_blk = lax.axis_index("blk")
    sub_dev = activity.shape[0]
    trials = activity.shape[2]
    quarter = activity.shape[3]
    slot_cap = slot_src.shape[0]
    sub_width = weights.shape[3]
    offsets = (-1, 1, n_areas // 2)

    occupied = jnp.arange(slot_cap) < slot_count[0]
    select = ((slot_dst[:, None] == jnp.arange(sub_dev)[None, :]) & occupied[:, None]).astype(jnp.float32)

    wanted = jnp.clip(slot_src % sub_dev, 0, sub_dev - 1).astype(jnp.int32)
    provide = []
    for k in range(slot_cap):
        perm = [(i, (i + offsets[k]) % n_areas) for i in range(n_areas)]
        provide.append(lax.ppermute(wanted[k], "area", perm))
    provide = jnp.stack(provide)
    select_provided = ((slot_dst[:, None] == provide[None, :]) & occupied[:, None]).astype(jnp.float32)

    own_state = jnp.stack([activity[:, 0], ext_input[:, 0].astype(jnp.float32)])

    def gather_blk(x):
        copies = jnp.broadcast_to(x[None], (n_blk,) + x.shape)
        return lax.all_to_all(copies, "blk", split_axis=0, concat_axis=0, tiled=True)

    state_parts = gather_blk(own_state)

    def pick(x, idx):
        return jnp.stack([lax.dynamic_index_in_dim(x, idx[k], 0, keepdims=False) for k in range(slot_cap)])

    provide_hot = provide[:, None] == jnp.arange(sub_dev)[None, :]

    def pick_hot(x):
        return jnp.sum(jnp.where(provide_hot[:, :, None, None], x[None], jnp.zeros((), x.dtype)), axis=1)

    state_full = state_parts.transpose(1, 2, 3, 0, 4).reshape(2, sub_dev, trials, sub_width)
    current = state_full[0]
    drive_in = state_full[1]
    drive_provided = pick(drive_in, provide)
    first_act = jnp.stack([pick_hot(state_parts[j, 0]) for j in range(n_blk)], axis=2)
    first_act = first_act.reshape(slot_cap, trials, sub_width)

    def advance(cur, contrib, sel, drive):
        summed = sum(sel[k][:, None, None] * contrib[k][None] for k in range(slot_cap))
        return cur + euler_step * (summed - cur + drive)

    def exchange(payload):
        got = []
        for k in range(slot_cap):
            perm = [(i, (i - offsets[k]) % n_areas) for i in range(n_areas)]
            got.append(lax.ppermute(payload[k], "area", perm))
        return jnp.stack(got)

    payload = jnp.tanh(first_act).astype(jnp.bfloat16)
    own_w, payload = lax.optimization_barrier((weights[:, 0], payload))
    w_parts = gather_blk(own_w)
    w_full = w_parts.transpose(1, 0, 2, 3).reshape(slot_cap, sub_width, sub_width)
    pre_list = []
    post_list = []
    for step_idx in range(STEPS):
        presyn = exchange(payload)
        contrib = jnp.einsum("knu,kuv->knv", presyn, w_full, preferred_element_type=jnp.float32)
        if step_idx + 1 < STEPS:
            provided_now = advance(pick(current, provide), contrib, select_provided, drive_provided)
            payload = jnp.tanh(provided_now).astype(jnp.bfloat16)
        current = advance(current, contrib, select, drive_in)
        pre_list.append(lax.dynamic_slice_in_dim(presyn, my_blk * quarter, quarter, 2))
        post_list.append(jnp.tanh(pick(current, slot_dst)).astype(jnp.bfloat16))
    final_state = lax.dynamic_slice_in_dim(current, my_blk * quarter, quarter, 2)[:, None]

    pre_centered = centre(jnp.stack(pre_list, axis=1))
    post_centered = centre(jnp.stack(post_list, axis=1))
    change = jnp.einsum("ktnq,ktnu->kqu", pre_centered, post_centered, preferred_element_type=jnp.float32)
    gate_on = (occupied & (hebb_mask == 1)).astype(jnp.float32)
    norm_scale = (STEPS * trials) ** (-0.5)
    plasticity = (change * gate_on[:, None, None] * norm_scale).astype(jnp.bfloat16)[:, None]
    return (final_state, plasticity)


def solution(mesh):
    in_specs = (
        P("area", "blk", None, None),
        P("area", "blk", None, None),
        P("area", "blk", None, None),
        P("area"),
        P("area"),
        P("area"),
        P("area"),
    )
    out_specs = (P("area", "blk", None, None), P("area", "blk", None, None))
    return jax.shard_map(body, mesh=mesh, in_specs=in_specs, out_specs=out_specs, check_vma=False)
```

```python
import jax
import jax.numpy as jnp
from jax import lax
from jax.sharding import PartitionSpec as P


STEPS = 4


euler_step = 0.5


def centre(x):
    xf = x.astype(jnp.float32)
    return (xf - jnp.mean(xf, axis=-2, keepdims=True)).astype(jnp.bfloat16)


def step_body(activity, ext_input, weights, slot_dst, slot_src, slot_count, hebb_mask):
    n_areas = lax.axis_size("area")
    n_blk = lax.axis_size("blk")
    my_blk = lax.axis_index("blk")
    sub_dev = activity.shape[0]
    trials = activity.shape[2]
    quarter = activity.shape[3]
    slot_cap = slot_src.shape[0]
    sub_width = weights.shape[3]
    offsets = (-1, 1, n_areas // 2)

    occupied = jnp.arange(slot_cap) < slot_count[0]
    select = ((slot_dst[:, None] == jnp.arange(sub_dev)[None, :]) & occupied[:, None]).astype(jnp.float32)

    wanted = jnp.clip(slot_src % sub_dev, 0, sub_dev - 1).astype(jnp.int32)
    provide = []
    for k in range(slot_cap):
        perm = [(i, (i + offsets[k]) % n_areas) for i in range(n_areas)]
        provide.append(lax.ppermute(wanted[k], "area", perm))
    provide = jnp.stack(provide)
    select_provided = ((slot_dst[:, None] == provide[None, :]) & occupied[:, None]).astype(jnp.float32)

    own_state = activity[:, 0]

    def gather_blk(x):
        copies = jnp.broadcast_to(x[None], (n_blk,) + x.shape)
        return lax.all_to_all(copies, "blk", split_axis=0, concat_axis=0, tiled=True)

    state_parts = gather_blk(own_state)

    def pick(x, idx):
        return jnp.stack([lax.dynamic_index_in_dim(x, idx[k], 0, keepdims=False) for k in range(slot_cap)])

    provide_hot = provide[:, None] == jnp.arange(sub_dev)[None, :]

    def pick_hot(x):
        return jnp.sum(jnp.where(provide_hot[:, :, None, None], x[None], jnp.zeros((), x.dtype)), axis=1)

    current = state_parts.transpose(1, 2, 0, 3).reshape(sub_dev, trials, sub_width)
    first_act = jnp.stack([pick_hot(state_parts[j]) for j in range(n_blk)], axis=2)
    first_act = first_act.reshape(slot_cap, trials, sub_width)

    def advance(cur, contrib, sel, drive):
        summed = sum(sel[k][:, None, None] * contrib[k][None] for k in range(slot_cap))
        return cur + euler_step * (summed - cur + drive)

    def exchange(payload):
        got = []
        for k in range(slot_cap):
            perm = [(i, (i - offsets[k]) % n_areas) for i in range(n_areas)]
            got.append(lax.ppermute(payload[k], "area", perm))
        return jnp.stack(got)

    payload = jnp.tanh(first_act).astype(jnp.bfloat16)
    own_w, own_ext, payload = lax.optimization_barrier((weights[:, 0], ext_input[:, 0], payload))
    w_parts = gather_blk(own_w)
    ext_parts = gather_blk(own_ext)
    drive_in = ext_parts.transpose(1, 2, 0, 3).reshape(sub_dev, trials, sub_width).astype(jnp.float32)
    drive_provided = pick(drive_in, provide)
    w_full = w_parts.transpose(1, 0, 2, 3).reshape(slot_cap, sub_width, sub_width)
    pre_list = []
    post_list = []
    for step_idx in range(STEPS):
        presyn = exchange(payload)
        contrib = jnp.einsum("knu,kuv->knv", presyn, w_full, preferred_element_type=jnp.float32)
        if step_idx + 1 < STEPS:
            provided_now = advance(pick(current, provide), contrib, select_provided, drive_provided)
            payload = jnp.tanh(provided_now).astype(jnp.bfloat16)
        current = advance(current, contrib, select, drive_in)
        pre_list.append(lax.dynamic_slice_in_dim(presyn, my_blk * quarter, quarter, 2))
        post_list.append(jnp.tanh(pick(current, slot_dst)).astype(jnp.bfloat16))
    final_state = lax.dynamic_slice_in_dim(current, my_blk * quarter, quarter, 2)[:, None]

    pre_centered = centre(jnp.stack(pre_list, axis=1))
    post_centered = centre(jnp.stack(post_list, axis=1))
    change = jnp.einsum("ktnq,ktnu->kqu", pre_centered, post_centered, preferred_element_type=jnp.float32)
    gate_on = (occupied & (hebb_mask == 1)).astype(jnp.float32)
    norm_scale = (STEPS * trials) ** (-0.5)
    plasticity = (change * gate_on[:, None, None] * norm_scale).astype(jnp.bfloat16)[:, None]
    return (final_state, plasticity)


def solution(mesh):
    in_specs = (
        P("area", "blk", None, None),
        P("area", "blk", None, None),
        P("area", "blk", None, None),
        P("area"),
        P("area"),
        P("area"),
        P("area"),
    )
    out_specs = (P("area", "blk", None, None), P("area", "blk", None, None))
    return jax.shard_map(step_body, mesh=mesh, in_specs=in_specs, out_specs=out_specs, check_vma=False)
```

```python
import jax
import jax.numpy as jnp
from jax import lax
from jax.sharding import PartitionSpec as P

STEPS = 4


euler_step = 0.5


def centre(x):
    xf = x.astype(jnp.float32)
    return (xf - jnp.mean(xf, axis=-2, keepdims=True)).astype(jnp.bfloat16)


def body(activity, ext_input, weights, slot_dst, slot_src, slot_count, hebb_mask):
    n_areas = lax.axis_size("area")
    n_blk = lax.axis_size("blk")
    my_blk = lax.axis_index("blk")
    sub_dev = activity.shape[0]
    trials = activity.shape[2]
    quarter = activity.shape[3]
    slot_cap = slot_src.shape[0]
    sub_width = weights.shape[3]
    offsets = (-1, 1, n_areas // 2)

    occupied = jnp.arange(slot_cap) < slot_count[0]
    select = ((slot_dst[:, None] == jnp.arange(sub_dev)[None, :]) & occupied[:, None]).astype(jnp.float32)

    wanted = jnp.clip(slot_src % sub_dev, 0, sub_dev - 1).astype(jnp.int32)
    provide = []
    for k in range(slot_cap):
        perm = [(i, (i + offsets[k]) % n_areas) for i in range(n_areas)]
        provide.append(lax.ppermute(wanted[k], "area", perm))
    provide = jnp.stack(provide)
    select_provided = ((slot_dst[:, None] == provide[None, :]) & occupied[:, None]).astype(jnp.float32)

    own_state = activity[:, 0]

    def gather_blk(x):
        copies = jnp.broadcast_to(x[None], (n_blk,) + x.shape)
        return lax.all_to_all(copies, "blk", split_axis=0, concat_axis=0, tiled=True)

    state_parts = gather_blk(own_state)

    def pick(x, idx):
        return jnp.stack([lax.dynamic_index_in_dim(x, idx[k], 0, keepdims=False) for k in range(slot_cap)])

    provide_hot = provide[:, None] == jnp.arange(sub_dev)[None, :]

    def pick_hot(x):
        return jnp.sum(jnp.where(provide_hot[:, :, None, None], x[None], jnp.zeros((), x.dtype)), axis=1)

    current = state_parts.transpose(1, 2, 0, 3).reshape(sub_dev, trials, sub_width)
    first_act = jnp.stack([pick_hot(state_parts[j]) for j in range(n_blk)], axis=2)
    first_act = first_act.reshape(slot_cap, trials, sub_width)

    def advance(cur, contrib, sel, drive):
        summed = sum(sel[k][:, None, None] * contrib[k][None] for k in range(slot_cap))
        return cur + euler_step * (summed - cur + drive)

    def exchange(payload):
        got = []
        for k in range(slot_cap):
            perm = [(i, (i - offsets[k]) % n_areas) for i in range(n_areas)]
            got.append(lax.ppermute(payload[k], "area", perm))
        return jnp.stack(got)

    payload = jnp.tanh(first_act).astype(jnp.bfloat16)
    own_w, own_ext, payload = lax.optimization_barrier((weights[:, 0], ext_input[:, 0], payload))
    w_size = own_w.size
    packed = gather_blk(jnp.concatenate([own_w.reshape(-1), own_ext.reshape(-1)]))
    w_parts = packed[:, :w_size].reshape((n_blk,) + own_w.shape)
    ext_parts = packed[:, w_size:].reshape((n_blk,) + own_ext.shape)
    drive_in = ext_parts.transpose(1, 2, 0, 3).reshape(sub_dev, trials, sub_width).astype(jnp.float32)
    drive_provided = pick(drive_in, provide)
    w_full = w_parts.transpose(1, 0, 2, 3).reshape(slot_cap, sub_width, sub_width)
    pre_list = []
    post_list = []
    for step_idx in range(STEPS):
        presyn = exchange(payload)
        contrib = jnp.einsum("knu,kuv->knv", presyn, w_full, preferred_element_type=jnp.float32)
        if step_idx + 1 < STEPS:
            provided_now = advance(pick(current, provide), contrib, select_provided, drive_provided)
            payload = jnp.tanh(provided_now).astype(jnp.bfloat16)
        current = advance(current, contrib, select, drive_in)
        pre_list.append(lax.dynamic_slice_in_dim(presyn, my_blk * quarter, quarter, 2))
        post_list.append(jnp.tanh(pick(current, slot_dst)).astype(jnp.bfloat16))
    final_state = lax.dynamic_slice_in_dim(current, my_blk * quarter, quarter, 2)[:, None]

    pre_centered = centre(jnp.stack(pre_list, axis=1))
    post_centered = centre(jnp.stack(post_list, axis=1))
    change = jnp.einsum("ktnq,ktnu->kqu", pre_centered, post_centered, preferred_element_type=jnp.float32)
    gate_on = (occupied & (hebb_mask == 1)).astype(jnp.float32)
    norm_scale = (STEPS * trials) ** (-0.5)
    plasticity = (change * gate_on[:, None, None] * norm_scale).astype(jnp.bfloat16)[:, None]
    return (final_state, plasticity)


def solution(mesh):
    in_specs = (
        P("area", "blk", None, None),
        P("area", "blk", None, None),
        P("area", "blk", None, None),
        P("area"),
        P("area"),
        P("area"),
        P("area"),
    )
    out_specs = (P("area", "blk", None, None), P("area", "blk", None, None))
    return jax.shard_map(body, mesh=mesh, in_specs=in_specs, out_specs=out_specs, check_vma=False)
```

```python
import jax
import jax.numpy as jnp
from jax import lax
from jax.sharding import PartitionSpec as P

STEPS = 4


euler_step = 0.5


def centre(x):
    xf = x.astype(jnp.float32)
    return (xf - jnp.mean(xf, axis=-2, keepdims=True)).astype(jnp.bfloat16)


def body(activity, ext_input, weights, slot_dst, slot_src, slot_count, hebb_mask):
    n_areas = lax.axis_size("area")
    n_blk = lax.axis_size("blk")
    my_blk = lax.axis_index("blk")
    sub_dev = activity.shape[0]
    trials = activity.shape[2]
    quarter = activity.shape[3]
    slot_cap = slot_src.shape[0]
    sub_width = weights.shape[3]
    offsets = (-1, 1, n_areas // 2)

    occupied = jnp.arange(slot_cap) < slot_count[0]
    select = ((slot_dst[:, None] == jnp.arange(sub_dev)[None, :]) & occupied[:, None]).astype(jnp.float32)

    wanted = jnp.clip(slot_src % sub_dev, 0, sub_dev - 1).astype(jnp.int32)
    provide = []
    for k in range(slot_cap):
        perm = [(i, (i + offsets[k]) % n_areas) for i in range(n_areas)]
        provide.append(lax.ppermute(wanted[k], "area", perm))
    provide = jnp.stack(provide)
    select_provided = ((slot_dst[:, None] == provide[None, :]) & occupied[:, None]).astype(jnp.float32)

    own_state = activity[:, 0]

    def gather_blk(x):
        copies = jnp.broadcast_to(x[None], (n_blk,) + x.shape)
        return lax.all_to_all(copies, "blk", split_axis=0, concat_axis=0, tiled=True)

    state_parts = gather_blk(own_state)

    def pick(x, idx):
        return jnp.stack([lax.dynamic_index_in_dim(x, idx[k], 0, keepdims=False) for k in range(slot_cap)])

    provide_hot = provide[:, None] == jnp.arange(sub_dev)[None, :]

    def pick_hot(x):
        return jnp.sum(jnp.where(provide_hot[:, :, None, None], x[None], jnp.zeros((), x.dtype)), axis=1)

    current = state_parts.transpose(1, 2, 0, 3).reshape(sub_dev, trials, sub_width)
    first_act = jnp.stack([pick_hot(state_parts[j]) for j in range(n_blk)], axis=2)
    first_act = first_act.reshape(slot_cap, trials, sub_width)

    def advance(cur, contrib, sel, drive):
        summed = sum(sel[k][:, None, None] * contrib[k][None] for k in range(slot_cap))
        return cur + euler_step * (summed - cur + drive)

    def exchange(payload):
        got = []
        for k in range(slot_cap):
            perm = [(i, (i - offsets[k]) % n_areas) for i in range(n_areas)]
            got.append(lax.ppermute(payload[k], "area", perm))
        return jnp.stack(got)

    payload = jnp.tanh(first_act).astype(jnp.bfloat16)
    own_w, own_ext, payload = lax.optimization_barrier((weights[:, 0], ext_input[:, 0], payload))
    ext_rows = own_ext.size // (quarter * sub_width)
    packed = jnp.concatenate([own_w, own_ext.reshape(ext_rows, quarter, sub_width)], axis=0)
    packed = gather_blk(packed)
    w_parts = packed[:, :slot_cap]
    ext_parts = packed[:, slot_cap:].reshape((n_blk,) + own_ext.shape)
    drive_in = ext_parts.transpose(1, 2, 0, 3).reshape(sub_dev, trials, sub_width).astype(jnp.float32)
    drive_provided = pick(drive_in, provide)
    w_full = w_parts.transpose(1, 0, 2, 3).reshape(slot_cap, sub_width, sub_width)
    pre_list = []
    post_list = []
    for step_idx in range(STEPS):
        presyn = exchange(payload)
        contrib = jnp.einsum("knu,kuv->knv", presyn, w_full, preferred_element_type=jnp.float32)
        if step_idx + 1 < STEPS:
            provided_now = advance(pick(current, provide), contrib, select_provided, drive_provided)
            payload = jnp.tanh(provided_now).astype(jnp.bfloat16)
        current = advance(current, contrib, select, drive_in)
        pre_list.append(lax.dynamic_slice_in_dim(presyn, my_blk * quarter, quarter, 2))
        post_list.append(jnp.tanh(pick(current, slot_dst)).astype(jnp.bfloat16))
    final_state = lax.dynamic_slice_in_dim(current, my_blk * quarter, quarter, 2)[:, None]

    pre_centered = centre(jnp.stack(pre_list, axis=1))
    post_centered = centre(jnp.stack(post_list, axis=1))
    change = jnp.einsum("ktnq,ktnu->kqu", pre_centered, post_centered, preferred_element_type=jnp.float32)
    gate_on = (occupied & (hebb_mask == 1)).astype(jnp.float32)
    norm_scale = (STEPS * trials) ** (-0.5)
    plasticity = (change * gate_on[:, None, None] * norm_scale).astype(jnp.bfloat16)[:, None]
    return (final_state, plasticity)


def solution(mesh):
    in_specs = (
        P("area", "blk", None, None),
        P("area", "blk", None, None),
        P("area", "blk", None, None),
        P("area"),
        P("area"),
        P("area"),
        P("area"),
    )
    out_specs = (P("area", "blk", None, None), P("area", "blk", None, None))
    return jax.shard_map(body, mesh=mesh, in_specs=in_specs, out_specs=out_specs, check_vma=False)
```

```python
import jax
import jax.numpy as jnp
from jax import lax
from jax.sharding import PartitionSpec as P

STEPS = 4


euler_step = 0.5


def centre(x):
    xf = x.astype(jnp.float32)
    return (xf - jnp.mean(xf, axis=-2, keepdims=True)).astype(jnp.bfloat16)


def body(activity, ext_input, weights, slot_dst, slot_src, slot_count, hebb_mask):
    n_areas = lax.axis_size("area")
    n_blk = lax.axis_size("blk")
    my_blk = lax.axis_index("blk")
    sub_dev = activity.shape[0]
    trials = activity.shape[2]
    quarter = activity.shape[3]
    slot_cap = slot_src.shape[0]
    sub_width = weights.shape[3]
    offsets = (-1, 1, n_areas // 2)

    occupied = jnp.arange(slot_cap) < slot_count[0]
    select = ((slot_dst[:, None] == jnp.arange(sub_dev)[None, :]) & occupied[:, None]).astype(jnp.float32)

    wanted = jnp.clip(slot_src % sub_dev, 0, sub_dev - 1).astype(jnp.int32)
    provide = []
    for k in range(slot_cap):
        perm = [(i, (i + offsets[k]) % n_areas) for i in range(n_areas)]
        provide.append(lax.ppermute(wanted[k], "area", perm))
    provide = jnp.stack(provide)
    select_provided = ((slot_dst[:, None] == provide[None, :]) & occupied[:, None]).astype(jnp.float32)

    own_state = jnp.stack([activity[:, 0], ext_input[:, 0].astype(jnp.float32)])

    def gather_blk(x):
        copies = jnp.broadcast_to(x[None], (n_blk,) + x.shape)
        return lax.all_to_all(copies, "blk", split_axis=0, concat_axis=0, tiled=True)

    state_parts = gather_blk(own_state)

    def pick(x, idx):
        return jnp.stack([lax.dynamic_index_in_dim(x, idx[k], 0, keepdims=False) for k in range(slot_cap)])

    provide_hot = provide[:, None] == jnp.arange(sub_dev)[None, :]

    def pick_hot(x):
        return jnp.sum(jnp.where(provide_hot[:, :, None, None], x[None], jnp.zeros((), x.dtype)), axis=1)

    state_full = state_parts.transpose(1, 2, 3, 0, 4).reshape(2, sub_dev, trials, sub_width)
    current = state_full[0]
    drive_in = state_full[1]
    drive_provided = jnp.stack([pick_hot(state_parts[j, 1]) for j in range(n_blk)], axis=2)
    drive_provided = drive_provided.reshape(slot_cap, trials, sub_width)
    first_act = jnp.stack([pick_hot(state_parts[j, 0]) for j in range(n_blk)], axis=2)
    first_act = first_act.reshape(slot_cap, trials, sub_width)

    def advance(cur, contrib, sel, drive):
        summed = sum(sel[k][:, None, None] * contrib[k][None] for k in range(slot_cap))
        return cur + euler_step * (summed - cur + drive)

    def exchange(payload):
        got = []
        for k in range(slot_cap):
            perm = [(i, (i - offsets[k]) % n_areas) for i in range(n_areas)]
            got.append(lax.ppermute(payload[k], "area", perm))
        return jnp.stack(got)

    payload = jnp.tanh(first_act).astype(jnp.bfloat16)
    own_w, payload = lax.optimization_barrier((weights[:, 0], payload))
    w_parts = gather_blk(own_w)
    pre_list = []
    post_list = []
    for step_idx in range(STEPS):
        presyn = exchange(payload)
        presyn_parts = presyn.reshape(slot_cap, trials, n_blk, quarter)
        contrib = jnp.einsum("knjq,jkqv->knv", presyn_parts, w_parts, preferred_element_type=jnp.float32)
        if step_idx + 1 < STEPS:
            provided_before = first_act if step_idx == 0 else pick(current, provide)
            provided_now = advance(provided_before, contrib, select_provided, drive_provided)
            payload = jnp.tanh(provided_now).astype(jnp.bfloat16)
        current = advance(current, contrib, select, drive_in)
        pre_list.append(lax.dynamic_slice_in_dim(presyn, my_blk * quarter, quarter, 2))
        post_list.append(jnp.tanh(pick(current, slot_dst)).astype(jnp.bfloat16))
    final_state = lax.dynamic_slice_in_dim(current, my_blk * quarter, quarter, 2)[:, None]

    pre_centered = centre(jnp.stack(pre_list, axis=1))
    post_centered = centre(jnp.stack(post_list, axis=1))
    change = jnp.einsum("ktnq,ktnu->kqu", pre_centered, post_centered, preferred_element_type=jnp.float32)
    gate_on = (occupied & (hebb_mask == 1)).astype(jnp.float32)
    norm_scale = (STEPS * trials) ** (-0.5)
    plasticity = (change * gate_on[:, None, None] * norm_scale).astype(jnp.bfloat16)[:, None]
    return (final_state, plasticity)


def solution(mesh):
    in_specs = (
        P("area", "blk", None, None),
        P("area", "blk", None, None),
        P("area", "blk", None, None),
        P("area"),
        P("area"),
        P("area"),
        P("area"),
    )
    out_specs = (P("area", "blk", None, None), P("area", "blk", None, None))
    return jax.shard_map(body, mesh=mesh, in_specs=in_specs, out_specs=out_specs, check_vma=False)
```

```python
import jax
import jax.numpy as jnp
from jax import lax
from jax.sharding import PartitionSpec as P

STEPS = 4


euler_step = 0.5


def centre(x):
    xf = x.astype(jnp.float32)
    return (xf - jnp.mean(xf, axis=-2, keepdims=True)).astype(jnp.bfloat16)


def body(activity, ext_input, weights, slot_dst, slot_src, slot_count, hebb_mask):
    n_areas = lax.axis_size("area")
    n_blk = lax.axis_size("blk")
    my_blk = lax.axis_index("blk")
    sub_dev = activity.shape[0]
    trials = activity.shape[2]
    quarter = activity.shape[3]
    slot_cap = slot_src.shape[0]
    sub_width = weights.shape[3]
    offsets = (-1, 1, n_areas // 2)

    occupied = jnp.arange(slot_cap) < slot_count[0]
    select = ((slot_dst[:, None] == jnp.arange(sub_dev)[None, :]) & occupied[:, None]).astype(jnp.float32)

    wanted = jnp.clip(slot_src % sub_dev, 0, sub_dev - 1).astype(jnp.int32)
    provide = []
    for k in range(slot_cap):
        perm = [(i, (i + offsets[k]) % n_areas) for i in range(n_areas)]
        provide.append(lax.ppermute(wanted[k], "area", perm))
    provide = jnp.stack(provide)
    select_provided = ((slot_dst[:, None] == provide[None, :]) & occupied[:, None]).astype(jnp.float32)

    own_state = jnp.stack([activity[:, 0], ext_input[:, 0].astype(jnp.float32)])

    def gather_blk(x):
        copies = jnp.broadcast_to(x[None], (n_blk,) + x.shape)
        return lax.all_to_all(copies, "blk", split_axis=0, concat_axis=0, tiled=True)

    state_parts = gather_blk(own_state)

    def pick(x, idx):
        return jnp.stack([lax.dynamic_index_in_dim(x, idx[k], 0, keepdims=False) for k in range(slot_cap)])

    provide_hot = provide[:, None] == jnp.arange(sub_dev)[None, :]

    def pick_hot(x):
        return jnp.sum(jnp.where(provide_hot[:, :, None, None], x[None], jnp.zeros((), x.dtype)), axis=1)

    state_full = state_parts.transpose(1, 2, 3, 0, 4).reshape(2, sub_dev, trials, sub_width)
    current = state_full[0]
    drive_in = state_full[1]
    drive_provided = jnp.stack([pick_hot(state_parts[j, 1]) for j in range(n_blk)], axis=2)
    drive_provided = drive_provided.reshape(slot_cap, trials, sub_width)
    first_act = jnp.stack([pick_hot(state_parts[j, 0]) for j in range(n_blk)], axis=2)
    first_act = first_act.reshape(slot_cap, trials, sub_width)

    def advance(cur, contrib, sel, drive):
        summed = sum(sel[k][:, None, None] * contrib[k][None] for k in range(slot_cap))
        return cur + euler_step * (summed - cur + drive)

    def exchange(payload):
        got = []
        for k in range(slot_cap):
            perm = [(i, (i - offsets[k]) % n_areas) for i in range(n_areas)]
            got.append(lax.ppermute(payload[k], "area", perm))
        return jnp.stack(got)

    payload = jnp.tanh(first_act).astype(jnp.bfloat16)
    own_w, payload = lax.optimization_barrier((weights[:, 0], payload))
    w_parts = gather_blk(own_w)
    w_full = w_parts.transpose(1, 0, 2, 3).reshape(slot_cap, sub_width, sub_width)
    pre_list = []
    post_list = []
    for step_idx in range(STEPS):
        presyn = exchange(payload)
        contrib = jnp.einsum("knu,kuv->knv", presyn, w_full, preferred_element_type=jnp.float32)
        if step_idx + 1 < STEPS:
            provided_before = first_act if step_idx == 0 else pick(current, provide)
            provided_now = advance(provided_before, contrib, select_provided, drive_provided)
            payload = jnp.tanh(provided_now).astype(jnp.bfloat16)
        current = advance(current, contrib, select, drive_in)
        pre_list.append(lax.dynamic_slice_in_dim(presyn, my_blk * quarter, quarter, 2))
        post_list.append(jnp.tanh(pick(current, slot_dst)).astype(jnp.bfloat16))
    final_state = lax.dynamic_slice_in_dim(current, my_blk * quarter, quarter, 2)[:, None]

    pre_centered = centre(jnp.stack(pre_list, axis=1))
    post_centered = centre(jnp.stack(post_list, axis=1))
    change = jnp.einsum("ktnq,ktnu->kqu", pre_centered, post_centered, preferred_element_type=jnp.float32)
    gate_on = (occupied & (hebb_mask == 1)).astype(jnp.float32)
    norm_scale = (STEPS * trials) ** (-0.5)
    plasticity = (change * gate_on[:, None, None] * norm_scale).astype(jnp.bfloat16)[:, None]
    return (final_state, plasticity)


def solution(mesh):
    in_specs = (
        P("area", "blk", None, None),
        P("area", "blk", None, None),
        P("area", "blk", None, None),
        P("area"),
        P("area"),
        P("area"),
        P("area"),
    )
    out_specs = (P("area", "blk", None, None), P("area", "blk", None, None))
    return jax.shard_map(body, mesh=mesh, in_specs=in_specs, out_specs=out_specs, check_vma=False)
```

```python
import jax
import jax.numpy as jnp
from jax import lax
from jax.sharding import PartitionSpec as P


STEPS = 4


euler_step = 0.5


def centre(x):
    xf = x.astype(jnp.float32)
    return (xf - jnp.mean(xf, axis=-2, keepdims=True)).astype(jnp.bfloat16)


def step_body(activity, ext_input, weights, slot_dst, slot_src, slot_count, hebb_mask):
    n_areas = lax.axis_size("area")
    n_blk = lax.axis_size("blk")
    my_blk = lax.axis_index("blk")
    sub_dev = activity.shape[0]
    trials = activity.shape[2]
    quarter = activity.shape[3]
    slot_cap = slot_src.shape[0]
    sub_width = weights.shape[3]
    offsets = (-1, 1, n_areas // 2)

    occupied = jnp.arange(slot_cap) < slot_count[0]
    select = ((slot_dst[:, None] == jnp.arange(sub_dev)[None, :]) & occupied[:, None]).astype(jnp.float32)

    wanted = jnp.clip(slot_src % sub_dev, 0, sub_dev - 1).astype(jnp.int32)
    provide = []
    for k in range(slot_cap):
        perm = [(i, (i + offsets[k]) % n_areas) for i in range(n_areas)]
        provide.append(lax.ppermute(wanted[k], "area", perm))
    provide = jnp.stack(provide)
    select_provided = ((slot_dst[:, None] == provide[None, :]) & occupied[:, None]).astype(jnp.float32)

    own_state = jnp.stack([activity[:, 0], ext_input[:, 0].astype(jnp.float32)])

    def gather_blk(x):
        copies = jnp.broadcast_to(x[None], (n_blk,) + x.shape)
        return lax.all_to_all(copies, "blk", split_axis=0, concat_axis=0, tiled=True)

    w_parts = gather_blk(weights[:, 0])
    state_parts = gather_blk(own_state)

    def pick(x, idx):
        return jnp.stack([lax.dynamic_index_in_dim(x, idx[k], 0, keepdims=False) for k in range(slot_cap)])

    provide_hot = provide[:, None] == jnp.arange(sub_dev)[None, :]

    def pick_hot(x):
        return jnp.sum(jnp.where(provide_hot[:, :, None, None], x[None], jnp.zeros((), x.dtype)), axis=1)

    state_full = state_parts.transpose(1, 2, 3, 0, 4).reshape(2, sub_dev, trials, sub_width)
    current = state_full[0]
    drive_in = state_full[1]
    drive_provided = pick(drive_in, provide)
    first_act = jnp.stack([pick_hot(state_parts[j, 0]) for j in range(n_blk)], axis=2)
    first_act = first_act.reshape(slot_cap, trials, sub_width)

    def advance(cur, contrib, sel, drive):
        summed = sum(sel[k][:, None, None] * contrib[k][None] for k in range(slot_cap))
        return cur + euler_step * (summed - cur + drive)

    def exchange(payload):
        got = []
        for k in range(slot_cap):
            perm = [(i, (i - offsets[k]) % n_areas) for i in range(n_areas)]
            got.append(lax.ppermute(payload[k], "area", perm))
        return jnp.stack(got)

    payload = jnp.tanh(first_act).astype(jnp.bfloat16)
    w_full = w_parts.transpose(1, 0, 2, 3).reshape(slot_cap, sub_width, sub_width)
    pre_list = []
    post_list = []
    for step_idx in range(STEPS):
        presyn = exchange(payload)
        contrib = jnp.einsum("knu,kuv->knv", presyn, w_full, preferred_element_type=jnp.float32)
        if step_idx + 1 < STEPS:
            provided_now = advance(pick(current, provide), contrib, select_provided, drive_provided)
            payload = jnp.tanh(provided_now).astype(jnp.bfloat16)
        current = advance(current, contrib, select, drive_in)
        pre_list.append(lax.dynamic_slice_in_dim(presyn, my_blk * quarter, quarter, 2))
        post_list.append(jnp.tanh(pick(current, slot_dst)).astype(jnp.bfloat16))
    final_state = lax.dynamic_slice_in_dim(current, my_blk * quarter, quarter, 2)[:, None]

    pre_centered = centre(jnp.stack(pre_list, axis=1))
    post_centered = centre(jnp.stack(post_list, axis=1))
    change = jnp.einsum("ktnq,ktnu->kqu", pre_centered, post_centered, preferred_element_type=jnp.float32)
    gate_on = (occupied & (hebb_mask == 1)).astype(jnp.float32)
    norm_scale = (STEPS * trials) ** (-0.5)
    plasticity = (change * gate_on[:, None, None] * norm_scale).astype(jnp.bfloat16)[:, None]
    return (final_state, plasticity)


def solution(mesh):
    in_specs = (
        P("area", "blk", None, None),
        P("area", "blk", None, None),
        P("area", "blk", None, None),
        P("area"),
        P("area"),
        P("area"),
        P("area"),
    )
    out_specs = (P("area", "blk", None, None), P("area", "blk", None, None))
    return jax.shard_map(step_body, mesh=mesh, in_specs=in_specs, out_specs=out_specs, check_vma=False)
```
